32 devices in a mesh: groups: 2 (over y), col: 4 (over z), aux: 2 (over x), rep: 2 (over core).
Axes of the slice: x: 2, y: 2, z: 4, core: 2. Of those that a mesh axis runs over, the one named last changes fastest.
Arguments:
- b_aux: bfloat16 [4, 4096, 2400], P(('groups', 'aux'), ('col', 'rep')), parts along dimension 0, may hold values from -0.59765625 to 0.59765625
- occ_energies: float32 [2], P('groups'), parts along dimension 0, may hold values from -2 to -0.3
- vir_energies: float32 [4800], P('groups'), parts along dimension 0, may hold values from 0.2 to 3
- owners: int32 [2], replicated, may hold values from 0 to 7
Outputs:
- gamma: float32 [4, 4096, 2400], P(('groups', 'aux'), None, ('col', 'rep')), parts along dimension 0
The draws below stay inside these ranges and needn't reach their ends.
There are 2 independent parts, one for each index of `groups`. The reference program is written for one: setup_inputs(seed, part) draws one part's arguments, and reference() takes and returns one part's arrays. A program takes and returns all parts, laid end to end along the dimension named above; an argument that names none is the same for every part. Nothing has to cross between parts.
Inputs may be any that keep to these rules, and one draw needn't show every extreme that they name: owners[s] is a column shard index in the order of col+rep; owners may repeat.
All inputs are finite; a program needn't handle non-finite values.
Results may differ from the reference program's by a relative error of at most 0.003.
Values may be sent and summed in bfloat16 or wider, within the bound.
No kernel may reach another device: no remote copies, remote signals or barrier semaphores. Data moves between devices by JAX's collectives and lax.ppermute only.
A program may use at most 64 MiB of HBM per device.

```python
import jax
import jax.numpy as jnp
from jax import lax

NV = 2400
NAUX = 8192
COLS_DEV = 300
STEPS = 2
NCOL = 2400
NOCC = 1
AUX_BLK = 4096
N_COL = 4
N_AUX = 2
N_REP = 2


def block_scale(stream_key, dims, cuts, least, top_value):
    def one(axis_at, blocks):
        steps = jax.random.uniform(jax.random.fold_in(jax.random.fold_in(stream_key, 6), axis_at), (blocks,), jnp.float32, least / len(cuts), top_value / len(cuts))
        return jnp.repeat(jnp.exp(steps), dims[axis_at] // blocks).reshape((-1,) + (1,) * (len(dims) - axis_at - 1))

    loudness = one(*cuts[0])
    for cut in cuts[1:]:
        loudness = loudness * one(*cut)
    return loudness


def gaussian(stream_key, shape, scale, reach, split=(), kind=jnp.bfloat16):
    values = jax.random.normal(stream_key, shape, jnp.float32) * scale
    if len(split) > 0:
        values = block_scale(stream_key, shape, split, -0.22, 0.18) * values
    return jnp.clip(values, min=-reach, max=reach).astype(kind)


def setup_inputs(seed: int = 0, part: int = 0) -> dict:
    splits = jax.random.split(jax.random.key(seed), 5)
    part_keys = jax.random.split(jax.random.fold_in(splits[4], part), 5)
    return {
        "b_aux": gaussian(part_keys[0], (N_AUX, AUX_BLK, NCOL), 0.1, 0.59765625, ((0, 2), (1, 8))),
        "occ_energies": jnp.clip(jax.random.uniform(part_keys[1], (NOCC,), jnp.float32, -2.0, -0.3), -2.0, -0.3),
        "vir_energies": jnp.clip(jax.random.uniform(part_keys[2], (NV,), jnp.float32, 0.2, 3.0), 0.2, 3.0),
        "owners": jax.random.randint(splits[3], (STEPS,), 0, N_COL * N_REP).astype(jnp.int32),
    }


os_scale = 1.3


def reference(b_aux, occ_energies, vir_energies, owners):
    flat = b_aux.reshape(NAUX, NCOL)
    col_energy = (vir_energies[None, :] - occ_energies[:, None]).reshape(NCOL)
    gamma_acc = jnp.zeros((NAUX, NCOL), jnp.float32)
    for step_index in range(STEPS):
        first = (owners[step_index] * COLS_DEV).astype(jnp.int32)
        owner_cols = lax.dynamic_slice_in_dim(flat, first, COLS_DEV, 1)
        owner_energy = lax.dynamic_slice_in_dim(col_energy, first, COLS_DEV, 0)
        coupling = lax.dot_general(flat, owner_cols, (((0,), (0,)), ((), ())), preferred_element_type=jnp.float32)
        amplitude = (os_scale * coupling / (col_energy[:, None] + owner_energy[None, :])).astype(jnp.bfloat16)
        gamma_acc = gamma_acc + lax.dot_general(owner_cols, amplitude, (((1,), (1,)), ((), ())), preferred_element_type=jnp.float32)
    return gamma_acc.reshape(N_AUX, NAUX // N_AUX, NCOL)
```

```python
import jax
import jax.numpy as jnp
from jax import lax
from jax.sharding import PartitionSpec as P

os_scale = 1.3
COLS = ("col", "rep")
PARTIAL_BYTES_MAX = 16 * 2**20


def owner_columns(local, col_energy, owners, width):
    owned = []
    owner_energy = []
    for step_index in range(owners.shape[0]):
        first = owners[step_index] * width
        owned.append(lax.dynamic_slice_in_dim(local, first, width, 1))
        owner_energy.append(lax.dynamic_slice_in_dim(col_energy, first, width, 0))
    return jnp.concatenate(owned, axis=1), jnp.concatenate(owner_energy, axis=0)


def coupling_by_partials(local, owned, shards, width):
    rows = local.shape[0]
    blocked = local.reshape(rows, shards, width)
    partial_value = lax.dot_general(
        blocked, owned, (((0,), (0,)), ((), ())), preferred_element_type=jnp.float32
    )
    return lax.psum_scatter(partial_value, COLS, scatter_dimension=0, tiled=False)


def coupling_by_columns(b_aux, owned_all):
    moved = lax.all_to_all(b_aux, COLS, split_axis=2, concat_axis=1, tiled=True)
    return lax.dot_general(
        moved[0], owned_all, (((0,), (0,)), ((), ())), preferred_element_type=jnp.float32
    )


def body(b_aux, occ_energies, vir_energies, owners, *, shards, by_partials):
    local = b_aux[0]
    width = local.shape[1] // shards
    col_energy = (vir_energies[None, :] - occ_energies[:, None]).reshape(-1)
    shard_index = lax.axis_index(COLS)
    energy_mine = lax.dynamic_slice_in_dim(col_energy, shard_index * width, width, 0)
    owned, owner_energy = owner_columns(local, col_energy, owners, width)
    owned_all = lax.all_gather(owned, COLS, axis=0, tiled=True)
    if by_partials:
        coupling = coupling_by_partials(local, owned, shards, width)
    else:
        coupling = coupling_by_columns(b_aux, owned_all)
    coupling = lax.psum(coupling, "aux")
    denominator = energy_mine[:, None] + owner_energy[None, :]
    amplitude = (os_scale * coupling / denominator).astype(jnp.bfloat16)
    gamma = lax.dot_general(
        owned_all, amplitude, (((1,), (1,)), ((), ())), preferred_element_type=jnp.float32
    )
    return gamma[None]


def solution(mesh):
    shards = mesh.shape["col"] * mesh.shape["rep"]

    def run(b_aux, occ_energies, vir_energies, owners):
        ncol = b_aux.shape[2]
        partial_bytes = ncol * owners.shape[0] * (ncol // shards) * 4
        by_partials = partial_bytes <= PARTIAL_BYTES_MAX
        placed = (P(("groups", "aux"), COLS, None), P("groups"), P("groups"), P())
        return jax.shard_map(
            lambda *a: body(*a, shards=shards, by_partials=by_partials),
            mesh=mesh,
            in_specs=placed,
            out_specs=P(("groups", "aux"), None, COLS),
            check_vma=False,
        )(b_aux, occ_energies, vir_energies, owners)

    return run
```

```python
import jax
import jax.numpy as jnp
from jax import lax
from jax.sharding import PartitionSpec as P

os_scale = 1.3
COLS = ("col", "rep")
PARTIAL_BYTES_MAX = 16 * 2**20
LINE_MAX = 8


def owner_columns(local, col_energy, owners, width):
    owned = []
    owner_energy = []
    for step_index in range(owners.shape[0]):
        first = owners[step_index] * width
        owned.append(lax.dynamic_slice_in_dim(local, first, width, 1))
        owner_energy.append(lax.dynamic_slice_in_dim(col_energy, first, width, 0))
    return jnp.concatenate(owned, axis=1), jnp.concatenate(owner_energy, axis=0)


def coupling_by_partials(local, owned, shards, width):
    rows = local.shape[0]
    blocked = local.reshape(rows, shards, width)
    partial_value = lax.dot_general(
        blocked, owned, (((0,), (0,)), ((), ())), preferred_element_type=jnp.float32
    )
    return lax.psum_scatter(partial_value, COLS, scatter_dimension=0, tiled=False)


def coupling_by_columns(b_aux, owned_all):
    moved = lax.all_to_all(b_aux, COLS, split_axis=2, concat_axis=1, tiled=True)
    return lax.dot_general(
        moved[0], owned_all, (((0,), (0,)), ((), ())), preferred_element_type=jnp.float32
    )


def shift(value, axis, size, offset):
    pairs = [(i, i + offset) for i in range(size) if 0 <= i + offset < size]
    return lax.ppermute(value, axis, pairs)


def gather_line(owned, n_col, n_rep):
    rows = owned.shape[0]
    me = lax.axis_index("col")
    pad = n_col - 1
    slots = jnp.zeros((3 * n_col - 2, rows, owned.shape[1]), owned.dtype)
    slots = lax.dynamic_update_slice_in_dim(slots, owned[None], me + pad, 0)
    right = owned
    left = owned
    for step in range(1, n_col):
        right = shift(right, "col", n_col, 1)
        left = shift(left, "col", n_col, -1)
        slots = lax.dynamic_update_slice_in_dim(slots, right[None], me - step + pad, 0)
        slots = lax.dynamic_update_slice_in_dim(slots, left[None], me + step + pad, 0)
    mine = slots[pad : pad + n_col]
    rep = lax.axis_index("rep")
    full = jnp.zeros((n_col, n_rep) + owned.shape, owned.dtype)
    full = lax.dynamic_update_slice_in_dim(full, mine[:, None], rep, 1)
    for step in range(1, n_rep):
        other = lax.ppermute(mine, "rep", [(i, (i + step) % n_rep) for i in range(n_rep)])
        full = lax.dynamic_update_slice_in_dim(full, other[:, None], (rep - step) % n_rep, 1)
    return full.reshape(n_col * n_rep * rows, owned.shape[1])


def exchange_sum(value, axis, size):
    total = value
    for step in range(1, size):
        total = total + lax.ppermute(value, axis, [(i, (i + step) % size) for i in range(size)])
    return total


def body(b_aux, occ_energies, vir_energies, owners, *, n_col, n_rep, n_aux, by_partials):
    shards = n_col * n_rep
    local = b_aux[0]
    width = local.shape[1] // shards
    col_energy = (vir_energies[None, :] - occ_energies[:, None]).reshape(-1)
    shard_index = lax.axis_index(COLS)
    energy_mine = lax.dynamic_slice_in_dim(col_energy, shard_index * width, width, 0)
    owned, owner_energy = owner_columns(local, col_energy, owners, width)
    if n_col <= LINE_MAX:
        owned_all = gather_line(owned, n_col, n_rep)
    else:
        owned_all = lax.all_gather(owned, COLS, axis=0, tiled=True)
    if by_partials:
        coupling = coupling_by_partials(local, owned, shards, width)
    else:
        coupling = coupling_by_columns(b_aux, owned_all)
    coupling = exchange_sum(coupling, "aux", n_aux)
    denominator = energy_mine[:, None] + owner_energy[None, :]
    amplitude = (os_scale * coupling / denominator).astype(jnp.bfloat16)
    gamma = lax.dot_general(
        owned_all, amplitude, (((1,), (1,)), ((), ())), preferred_element_type=jnp.float32
    )
    return gamma[None]


def solution(mesh):
    n_col, n_rep, n_aux = mesh.shape["col"], mesh.shape["rep"], mesh.shape["aux"]
    shards = n_col * n_rep

    def run(b_aux, occ_energies, vir_energies, owners):
        ncol = b_aux.shape[2]
        partial_bytes = ncol * owners.shape[0] * (ncol // shards) * 4
        by_partials = partial_bytes <= PARTIAL_BYTES_MAX
        placed = (P(("groups", "aux"), COLS, None), P("groups"), P("groups"), P())
        return jax.shard_map(
            lambda *a: body(*a, n_col=n_col, n_rep=n_rep, n_aux=n_aux, by_partials=by_partials),
            mesh=mesh,
            in_specs=placed,
            out_specs=P(("groups", "aux"), None, COLS),
            check_vma=False,
        )(b_aux, occ_energies, vir_energies, owners)

    return run
```

```python
import jax
import jax.numpy as jnp
from jax import lax
from jax.sharding import PartitionSpec as P

os_scale = 1.3
COLS = ("col", "rep")
PARTIAL_BYTES_MAX = 16 * 2**20


def owner_columns(local, col_energy, owners, width):
    owned = []
    owner_energy = []
    for step_index in range(owners.shape[0]):
        first = owners[step_index] * width
        owned.append(lax.dynamic_slice_in_dim(local, first, width, 1))
        owner_energy.append(lax.dynamic_slice_in_dim(col_energy, first, width, 0))
    return jnp.concatenate(owned, axis=1), jnp.concatenate(owner_energy, axis=0)


def coupling_by_partials(local, owned, shards, width):
    rows = local.shape[0]
    blocked = local.reshape(rows, shards, width)
    partial_value = lax.dot_general(
        blocked, owned, (((0,), (0,)), ((), ())), preferred_element_type=jnp.float32
    )
    return lax.psum_scatter(partial_value, COLS, scatter_dimension=0, tiled=False)


def coupling_by_columns(b_aux, owned_all):
    moved = lax.all_to_all(b_aux, COLS, split_axis=2, concat_axis=1, tiled=True)
    return lax.dot_general(
        moved[0], owned_all, (((0,), (0,)), ((), ())), preferred_element_type=jnp.float32
    )


def exchange_sum(value, axis, size):
    total = value
    for step in range(1, size):
        total = total + lax.ppermute(value, axis, [(i, (i + step) % size) for i in range(size)])
    return total


def body(b_aux, occ_energies, vir_energies, owners, *, shards, n_aux, by_partials):
    local = b_aux[0]
    width = local.shape[1] // shards
    col_energy = (vir_energies[None, :] - occ_energies[:, None]).reshape(-1)
    shard_index = lax.axis_index(COLS)
    energy_mine = lax.dynamic_slice_in_dim(col_energy, shard_index * width, width, 0)
    owned, owner_energy = owner_columns(local, col_energy, owners, width)
    owned_all = lax.all_gather(owned, COLS, axis=0, tiled=True)
    if by_partials:
        coupling = coupling_by_partials(local, owned, shards, width)
    else:
        coupling = coupling_by_columns(b_aux, owned_all)
    coupling = exchange_sum(coupling, "aux", n_aux)
    denominator = energy_mine[:, None] + owner_energy[None, :]
    amplitude = (os_scale * coupling / denominator).astype(jnp.bfloat16)
    gamma = lax.dot_general(
        owned_all, amplitude, (((1,), (1,)), ((), ())), preferred_element_type=jnp.float32
    )
    return gamma[None]


def solution(mesh):
    shards = mesh.shape["col"] * mesh.shape["rep"]

    def run(b_aux, occ_energies, vir_energies, owners):
        ncol = b_aux.shape[2]
        partial_bytes = ncol * owners.shape[0] * (ncol // shards) * 4
        by_partials = partial_bytes <= PARTIAL_BYTES_MAX
        placed = (P(("groups", "aux"), COLS, None), P("groups"), P("groups"), P())
        return jax.shard_map(
            lambda *a: body(*a, shards=shards, n_aux=mesh.shape["aux"], by_partials=by_partials),
            mesh=mesh,
            in_specs=placed,
            out_specs=P(("groups", "aux"), None, COLS),
            check_vma=False,
        )(b_aux, occ_energies, vir_energies, owners)

    return run
```

```python
import jax
import jax.numpy as jnp
from jax import lax
from jax.sharding import PartitionSpec as P

os_scale = 1.3
COLS = ("col", "rep")
PARTIAL_BYTES_MAX = 16 * 2**20
LINE_MAX = 8


def owner_columns(local, col_energy, owners, width):
    owned = []
    owner_energy = []
    for step_index in range(owners.shape[0]):
        first = owners[step_index] * width
        owned.append(lax.dynamic_slice_in_dim(local, first, width, 1))
        owner_energy.append(lax.dynamic_slice_in_dim(col_energy, first, width, 0))
    return jnp.concatenate(owned, axis=1), jnp.concatenate(owner_energy, axis=0)


def pick(stack, index):
    return lax.dynamic_index_in_dim(stack, index, 0, keepdims=False)


def line_reduce_scatter(partial_value, n_col, n_rep):
    me = lax.axis_index("col")
    rep = lax.axis_index("rep")
    summed = pick(partial_value, rep)
    for step in range(1, n_rep):
        pairs = [(i, (i + step) % n_rep) for i in range(n_rep)]
        summed = summed + lax.ppermute(pick(partial_value, (rep + step) % n_rep), "rep", pairs)
    right = None
    left = None
    for step in range(1, n_col):
        far = jnp.minimum(me + n_col - step, n_col - 1)
        message = pick(summed, far) if right is None else pick(summed, far) + right
        right = lax.ppermute(message, "col", [(c, c + 1) for c in range(step)])
        near = jnp.maximum(me - n_col + step, 0)
        message = pick(summed, near) if left is None else pick(summed, near) + left
        left = lax.ppermute(message, "col", [(c, c - 1) for c in range(n_col - step, n_col)])
    total = pick(summed, me)
    if right is not None:
        total = total + right + left
    return total


def line_all_gather(owned, n_col, n_rep):
    me = lax.axis_index("col")
    rep = lax.axis_index("rep")
    from_right = [None]
    from_left = [None]
    right = owned
    left = owned
    for step in range(1, n_col):
        right = lax.ppermute(right, "col", [(c, c + 1) for c in range(step - 1, n_col - 1)])
        left = lax.ppermute(left, "col", [(c, c - 1) for c in range(1, n_col - step + 1)])
        from_right.append(right)
        from_left.append(left)
    relative = [owned]
    for step in range(1, n_col):
        relative.append(jnp.where(me + step < n_col, from_left[step], from_right[n_col - step]))
    relative = jnp.stack(relative + relative)
    mine = lax.dynamic_slice_in_dim(relative, (n_col - me) % n_col, n_col, 0)
    by_offset = [mine]
    for step in range(1, n_rep):
        pairs = [(i, (i - step) % n_rep) for i in range(n_rep)]
        by_offset.append(lax.ppermute(mine, "rep", pairs))
    slots = []
    for slot in range(n_rep):
        value = by_offset[0]
        for step in range(1, n_rep):
            value = jnp.where((rep + step) % n_rep == slot, by_offset[step], value)
        slots.append(value)
    full = jnp.stack(slots, axis=1)
    return full.reshape((-1,) + owned.shape[1:])


def coupling_by_partials(local, owned, n_col, n_rep, width):
    rows = local.shape[0]
    blocked = local.reshape(rows, n_col, n_rep, width).transpose(0, 2, 1, 3)
    partial_value = lax.dot_general(
        blocked, owned, (((0,), (0,)), ((), ())), preferred_element_type=jnp.float32
    )
    return line_reduce_scatter(partial_value, n_col, n_rep)


def coupling_by_columns(b_aux, owned_all):
    moved = lax.all_to_all(b_aux, COLS, split_axis=2, concat_axis=1, tiled=True)
    return lax.dot_general(
        moved[0], owned_all, (((0,), (0,)), ((), ())), preferred_element_type=jnp.float32
    )


def exchange_sum(value, axis, size):
    total = value
    for step in range(1, size):
        total = total + lax.ppermute(value, axis, [(i, (i + step) % size) for i in range(size)])
    return total


def body(b_aux, occ_energies, vir_energies, owners, *, n_col, n_rep, n_aux, by_partials):
    shards = n_col * n_rep
    local = b_aux[0]
    width = local.shape[1] // shards
    col_energy = (vir_energies[None, :] - occ_energies[:, None]).reshape(-1)
    shard_index = lax.axis_index(COLS)
    energy_mine = lax.dynamic_slice_in_dim(col_energy, shard_index * width, width, 0)
    owned, owner_energy = owner_columns(local, col_energy, owners, width)
    if n_col <= LINE_MAX:
        owned_all = line_all_gather(owned, n_col, n_rep)
    else:
        owned_all = lax.all_gather(owned, COLS, axis=0, tiled=True)
    if by_partials:
        coupling = coupling_by_partials(local, owned, n_col, n_rep, width)
    else:
        coupling = coupling_by_columns(b_aux, owned_all)
    coupling = exchange_sum(coupling, "aux", n_aux)
    denominator = energy_mine[:, None] + owner_energy[None, :]
    amplitude = (os_scale * coupling / denominator).astype(jnp.bfloat16)
    gamma = lax.dot_general(
        owned_all, amplitude, (((1,), (1,)), ((), ())), preferred_element_type=jnp.float32
    )
    return gamma[None]


def solution(mesh):
    n_col, n_rep = mesh.shape["col"], mesh.shape["rep"]
    shards = n_col * n_rep

    def run(b_aux, occ_energies, vir_energies, owners):
        ncol = b_aux.shape[2]
        partial_bytes = ncol * owners.shape[0] * (ncol // shards) * 4
        by_partials = partial_bytes <= PARTIAL_BYTES_MAX
        placed = (P(("groups", "aux"), COLS, None), P("groups"), P("groups"), P())
        return jax.shard_map(
            lambda *a: body(*a, n_col=n_col, n_rep=n_rep, n_aux=mesh.shape["aux"], by_partials=by_partials),
            mesh=mesh,
            in_specs=placed,
            out_specs=P(("groups", "aux"), None, COLS),
            check_vma=False,
        )(b_aux, occ_energies, vir_energies, owners)

    return run
```

```python
import jax
import jax.numpy as jnp
from jax import lax
from jax.sharding import PartitionSpec as P

os_scale = 1.3
COLS = ("col", "rep")
PARTIAL_BYTES_MAX = 16 * 2**20


def owner_columns(local, col_energy, owners, width):
    owned = []
    owner_energy = []
    for step_index in range(owners.shape[0]):
        first = owners[step_index] * width
        owned.append(lax.dynamic_slice_in_dim(local, first, width, 1))
        owner_energy.append(lax.dynamic_slice_in_dim(col_energy, first, width, 0))
    return jnp.concatenate(owned, axis=1), jnp.concatenate(owner_energy, axis=0)


def coupling_by_partials(local, owned, n_col, n_rep, width):
    rows = local.shape[0]
    blocked = local.reshape(rows, n_col, n_rep, width).transpose(0, 2, 1, 3)
    partial_value = lax.dot_general(
        blocked, owned, (((0,), (0,)), ((), ())), preferred_element_type=jnp.float32
    )
    partial_value = lax.psum_scatter(partial_value, "rep", scatter_dimension=0, tiled=False)
    return lax.psum_scatter(partial_value, "col", scatter_dimension=0, tiled=False)


def gather_by_chip(owned):
    gathered = lax.all_gather(owned, "col", axis=0, tiled=False)
    gathered = lax.all_gather(gathered, "rep", axis=1, tiled=False)
    return gathered.reshape((-1,) + owned.shape[1:])


def coupling_by_columns(b_aux, owned_all):
    moved = lax.all_to_all(b_aux, COLS, split_axis=2, concat_axis=1, tiled=True)
    return lax.dot_general(
        moved[0], owned_all, (((0,), (0,)), ((), ())), preferred_element_type=jnp.float32
    )


def exchange_sum(value, axis, size):
    total = value
    for step in range(1, size):
        total = total + lax.ppermute(value, axis, [(i, (i + step) % size) for i in range(size)])
    return total


def body(b_aux, occ_energies, vir_energies, owners, *, n_col, n_rep, n_aux, by_partials):
    shards = n_col * n_rep
    local = b_aux[0]
    width = local.shape[1] // shards
    col_energy = (vir_energies[None, :] - occ_energies[:, None]).reshape(-1)
    shard_index = lax.axis_index(COLS)
    energy_mine = lax.dynamic_slice_in_dim(col_energy, shard_index * width, width, 0)
    owned, owner_energy = owner_columns(local, col_energy, owners, width)
    owned_all = gather_by_chip(owned)
    if by_partials:
        coupling = coupling_by_partials(local, owned, n_col, n_rep, width)
    else:
        coupling = coupling_by_columns(b_aux, owned_all)
    coupling = exchange_sum(coupling, "aux", n_aux)
    denominator = energy_mine[:, None] + owner_energy[None, :]
    amplitude = (os_scale * coupling / denominator).astype(jnp.bfloat16)
    gamma = lax.dot_general(
        owned_all, amplitude, (((1,), (1,)), ((), ())), preferred_element_type=jnp.float32
    )
    return gamma[None]


def solution(mesh):
    n_col, n_rep = mesh.shape["col"], mesh.shape["rep"]
    shards = n_col * n_rep

    def run(b_aux, occ_energies, vir_energies, owners):
        ncol = b_aux.shape[2]
        partial_bytes = ncol * owners.shape[0] * (ncol // shards) * 4
        by_partials = partial_bytes <= PARTIAL_BYTES_MAX
        placed = (P(("groups", "aux"), COLS, None), P("groups"), P("groups"), P())
        return jax.shard_map(
            lambda *a: body(*a, n_col=n_col, n_rep=n_rep, n_aux=mesh.shape["aux"], by_partials=by_partials),
            mesh=mesh,
            in_specs=placed,
            out_specs=P(("groups", "aux"), None, COLS),
            check_vma=False,
        )(b_aux, occ_energies, vir_energies, owners)

    return run
```

```python
import jax
import jax.numpy as jnp
from jax import lax
from jax.sharding import PartitionSpec as P

os_scale = 1.3
COLS = ("col", "rep")
PARTIAL_BYTES_MAX = 16 * 2**20


def owner_columns(local, col_energy, owners, width):
    owned = []
    owner_energy = []
    for step_index in range(owners.shape[0]):
        first = owners[step_index] * width
        owned.append(lax.dynamic_slice_in_dim(local, first, width, 1))
        owner_energy.append(lax.dynamic_slice_in_dim(col_energy, first, width, 0))
    return jnp.concatenate(owned, axis=1), jnp.concatenate(owner_energy, axis=0)


def coupling_by_partials(local, owned, shards, width):
    rows = local.shape[0]
    blocked = local.reshape(rows, shards, width)
    partial_value = lax.dot_general(
        blocked, owned, (((0,), (0,)), ((), ())), preferred_element_type=jnp.float32
    )
    return lax.psum_scatter(partial_value, COLS, scatter_dimension=0, tiled=False)


def coupling_by_columns(b_aux, owned_all):
    moved = lax.all_to_all(b_aux, COLS, split_axis=2, concat_axis=1, tiled=True)
    return lax.dot_general(
        moved[0], owned_all, (((0,), (0,)), ((), ())), preferred_element_type=jnp.float32
    )


def exchange_sum(value, axis, size):
    total = value
    for step in range(1, size):
        total = total + lax.ppermute(value, axis, [(i, (i + step) % size) for i in range(size)])
    return total


def gather_by_chip(owned):
    gathered = lax.all_gather(owned, "col", axis=0, tiled=False)
    gathered = lax.all_gather(gathered, "rep", axis=1, tiled=False)
    return gathered.reshape((-1,) + owned.shape[1:])


def body(b_aux, occ_energies, vir_energies, owners, *, shards, n_aux, by_partials):
    local = b_aux[0]
    width = local.shape[1] // shards
    col_energy = (vir_energies[None, :] - occ_energies[:, None]).reshape(-1)
    shard_index = lax.axis_index(COLS)
    energy_mine = lax.dynamic_slice_in_dim(col_energy, shard_index * width, width, 0)
    owned, owner_energy = owner_columns(local, col_energy, owners, width)
    owned_all = gather_by_chip(owned)
    if by_partials:
        coupling = coupling_by_partials(local, owned, shards, width)
    else:
        coupling = coupling_by_columns(b_aux, owned_all)
    coupling = exchange_sum(coupling, "aux", n_aux)
    denominator = energy_mine[:, None] + owner_energy[None, :]
    amplitude = (os_scale * coupling / denominator).astype(jnp.bfloat16)
    gamma = lax.dot_general(
        owned_all, amplitude, (((1,), (1,)), ((), ())), preferred_element_type=jnp.float32
    )
    return gamma[None]


def solution(mesh):
    shards = mesh.shape["col"] * mesh.shape["rep"]

    def run(b_aux, occ_energies, vir_energies, owners):
        ncol = b_aux.shape[2]
        partial_bytes = ncol * owners.shape[0] * (ncol // shards) * 4
        by_partials = partial_bytes <= PARTIAL_BYTES_MAX
        placed = (P(("groups", "aux"), COLS, None), P("groups"), P("groups"), P())
        return jax.shard_map(
            lambda *a: body(*a, shards=shards, n_aux=mesh.shape["aux"], by_partials=by_partials),
            mesh=mesh,
            in_specs=placed,
            out_specs=P(("groups", "aux"), None, COLS),
            check_vma=False,
        )(b_aux, occ_energies, vir_energies, owners)

    return run
```

```python
import jax
import jax.numpy as jnp
from jax import lax
from jax.experimental import pallas as pl
from jax.experimental.pallas import tpu as pltpu
from jax.sharding import PartitionSpec as P

os_scale = 1.3
COLS = ("col", "rep")
PARTIAL_BYTES_MAX = 16 * 2**20


def owner_columns(local, col_energy, owners, width):
    owned = []
    owner_energy = []
    for step_index in range(owners.shape[0]):
        first = owners[step_index] * width
        owned.append(lax.dynamic_slice_in_dim(local, first, width, 1))
        owner_energy.append(lax.dynamic_slice_in_dim(col_energy, first, width, 0))
    return jnp.concatenate(owned, axis=1), jnp.concatenate(owner_energy, axis=0)


def coupling_by_partials(local, owned, shards, width):
    rows = local.shape[0]
    blocked = local.reshape(rows, shards, width)
    partial_value = lax.dot_general(
        blocked, owned, (((0,), (0,)), ((), ())), preferred_element_type=jnp.float32
    )
    return lax.psum_scatter(partial_value, COLS, scatter_dimension=0, tiled=False)


def coupling_by_columns(b_aux, owned_all):
    moved = lax.all_to_all(b_aux, COLS, split_axis=2, concat_axis=1, tiled=True)
    return lax.dot_general(
        moved[0], owned_all, (((0,), (0,)), ((), ())), preferred_element_type=jnp.float32
    )


def exchange_sum(value, axis, size):
    total = value
    for step in range(1, size):
        total = total + lax.ppermute(value, axis, [(i, (i + step) % size) for i in range(size)])
    return total


def gamma_kernel(amp_ref, owned_ref, out_ref):
    out_ref[:, 0, :] = lax.dot_general(
        amp_ref[...], owned_ref[...], (((1,), (1,)), ((), ())), preferred_element_type=jnp.float32
    )


def gamma_rows_last(amplitude, owned_all):
    width = amplitude.shape[0]
    rows = owned_all.shape[0]
    out = pl.pallas_call(
        gamma_kernel,
        out_shape=jax.ShapeDtypeStruct((width, 1, rows), jnp.float32),
        in_specs=[pl.BlockSpec(memory_space=pltpu.VMEM)] * 2,
        out_specs=pl.BlockSpec(memory_space=pltpu.VMEM),
        compiler_params=pltpu.CompilerParams(vmem_limit_bytes=48 * 2**20),
    )(amplitude, owned_all)
    return out.transpose(1, 2, 0)


def body(b_aux, occ_energies, vir_energies, owners, *, shards, n_aux, by_partials):
    local = b_aux[0]
    width = local.shape[1] // shards
    col_energy = (vir_energies[None, :] - occ_energies[:, None]).reshape(-1)
    shard_index = lax.axis_index(COLS)
    energy_mine = lax.dynamic_slice_in_dim(col_energy, shard_index * width, width, 0)
    owned, owner_energy = owner_columns(local, col_energy, owners, width)
    owned_all = lax.all_gather(owned, COLS, axis=0, tiled=True)
    if by_partials:
        coupling = coupling_by_partials(local, owned, shards, width)
    else:
        coupling = coupling_by_columns(b_aux, owned_all)
    coupling = exchange_sum(coupling, "aux", n_aux)
    denominator = energy_mine[:, None] + owner_energy[None, :]
    amplitude = (os_scale * coupling / denominator).astype(jnp.bfloat16)
    return gamma_rows_last(amplitude, owned_all)


def solution(mesh):
    shards = mesh.shape["col"] * mesh.shape["rep"]

    def run(b_aux, occ_energies, vir_energies, owners):
        ncol = b_aux.shape[2]
        partial_bytes = ncol * owners.shape[0] * (ncol // shards) * 4
        by_partials = partial_bytes <= PARTIAL_BYTES_MAX
        placed = (P(("groups", "aux"), COLS, None), P("groups"), P("groups"), P())
        return jax.shard_map(
            lambda *a: body(*a, shards=shards, n_aux=mesh.shape["aux"], by_partials=by_partials),
            mesh=mesh,
            in_specs=placed,
            out_specs=P(("groups", "aux"), None, COLS),
            check_vma=False,
        )(b_aux, occ_energies, vir_energies, owners)

    return run
```

```python
import jax
import jax.numpy as jnp
from jax import lax
from jax.experimental import pallas as pl
from jax.experimental.pallas import tpu as pltpu
from jax.sharding import PartitionSpec as P

os_scale = 1.3
COLS = ("col", "rep")
PARTIAL_BYTES_MAX = 0


def owner_columns(local, col_energy, owners, width):
    owned = []
    owner_energy = []
    for step_index in range(owners.shape[0]):
        first = owners[step_index] * width
        owned.append(lax.dynamic_slice_in_dim(local, first, width, 1))
        owner_energy.append(lax.dynamic_slice_in_dim(col_energy, first, width, 0))
    return jnp.concatenate(owned, axis=1), jnp.concatenate(owner_energy, axis=0)


def coupling_by_partials(local, owned, shards, width):
    rows = local.shape[0]
    blocked = local.reshape(rows, shards, width)
    partial_value = lax.dot_general(
        blocked, owned, (((0,), (0,)), ((), ())), preferred_element_type=jnp.float32
    )
    return lax.psum_scatter(partial_value, COLS, scatter_dimension=0, tiled=False)


def coupling_by_columns(b_aux, owned_all):
    moved = lax.all_to_all(b_aux, COLS, split_axis=2, concat_axis=1, tiled=True)
    return lax.dot_general(
        moved[0], owned_all, (((0,), (0,)), ((), ())), preferred_element_type=jnp.float32
    )


def exchange_sum(value, axis, size):
    total = value
    for step in range(1, size):
        total = total + lax.ppermute(value, axis, [(i, (i + step) % size) for i in range(size)])
    return total


def gamma_kernel(amp_ref, owned_ref, out_ref):
    out_ref[:, 0, :] = lax.dot_general(
        amp_ref[...], owned_ref[...], (((1,), (1,)), ((), ())), preferred_element_type=jnp.float32
    )


def gamma_rows_last(amplitude, owned_all):
    width = amplitude.shape[0]
    rows = owned_all.shape[0]
    out = pl.pallas_call(
        gamma_kernel,
        out_shape=jax.ShapeDtypeStruct((width, 1, rows), jnp.float32),
        in_specs=[pl.BlockSpec(memory_space=pltpu.VMEM)] * 2,
        out_specs=pl.BlockSpec(memory_space=pltpu.VMEM),
        compiler_params=pltpu.CompilerParams(vmem_limit_bytes=48 * 2**20),
    )(amplitude, owned_all)
    return out.transpose(1, 2, 0)


def body(b_aux, occ_energies, vir_energies, owners, *, shards, n_aux, by_partials):
    local = b_aux[0]
    width = local.shape[1] // shards
    col_energy = (vir_energies[None, :] - occ_energies[:, None]).reshape(-1)
    shard_index = lax.axis_index(COLS)
    energy_mine = lax.dynamic_slice_in_dim(col_energy, shard_index * width, width, 0)
    owned, owner_energy = owner_columns(local, col_energy, owners, width)
    owned_all = lax.all_gather(owned, COLS, axis=0, tiled=True)
    if by_partials:
        coupling = coupling_by_partials(local, owned, shards, width)
    else:
        coupling = coupling_by_columns(b_aux, owned_all)
    coupling = exchange_sum(coupling, "aux", n_aux)
    denominator = energy_mine[:, None] + owner_energy[None, :]
    amplitude = (os_scale * coupling / denominator).astype(jnp.bfloat16)
    return gamma_rows_last(amplitude, owned_all)


def solution(mesh):
    shards = mesh.shape["col"] * mesh.shape["rep"]

    def run(b_aux, occ_energies, vir_energies, owners):
        ncol = b_aux.shape[2]
        partial_bytes = ncol * owners.shape[0] * (ncol // shards) * 4
        by_partials = partial_bytes <= PARTIAL_BYTES_MAX
        placed = (P(("groups", "aux"), COLS, None), P("groups"), P("groups"), P())
        return jax.shard_map(
            lambda *a: body(*a, shards=shards, n_aux=mesh.shape["aux"], by_partials=by_partials),
            mesh=mesh,
            in_specs=placed,
            out_specs=P(("groups", "aux"), None, COLS),
            check_vma=False,
        )(b_aux, occ_energies, vir_energies, owners)

    return run
```

```python
import jax
import jax.numpy as jnp
from jax import lax
from jax.experimental import pallas as pl
from jax.experimental.pallas import tpu as pltpu
from jax.sharding import PartitionSpec as P

os_scale = 1.3
COLS = ("col", "rep")
PARTIAL_BYTES_MAX = 0


def owner_columns(local, col_energy, owners, width):
    owned = []
    owner_energy = []
    for step_index in range(owners.shape[0]):
        first = owners[step_index] * width
        owned.append(lax.dynamic_slice_in_dim(local, first, width, 1))
        owner_energy.append(lax.dynamic_slice_in_dim(col_energy, first, width, 0))
    return jnp.concatenate(owned, axis=1), jnp.concatenate(owner_energy, axis=0)


def coupling_by_partials(local, owned, shards, width):
    rows = local.shape[0]
    blocked = local.reshape(rows, shards, width)
    partial_value = lax.dot_general(
        blocked, owned, (((0,), (0,)), ((), ())), preferred_element_type=jnp.float32
    )
    return lax.psum_scatter(partial_value, COLS, scatter_dimension=0, tiled=False)


def coupling_by_columns(local, owned_all, shards, width):
    rows = local.shape[0]
    blocked = local.reshape(rows, shards, width).transpose(1, 0, 2)
    moved = lax.all_to_all(blocked, COLS, split_axis=0, concat_axis=0, tiled=True)
    return lax.dot_general(
        moved.reshape(shards * rows, width), owned_all, (((0,), (0,)), ((), ())),
        preferred_element_type=jnp.float32,
    )


def exchange_sum(value, axis, size):
    total = value
    for step in range(1, size):
        total = total + lax.ppermute(value, axis, [(i, (i + step) % size) for i in range(size)])
    return total


def gamma_kernel(amp_ref, owned_ref, out_ref):
    out_ref[:, 0, :] = lax.dot_general(
        amp_ref[...], owned_ref[...], (((1,), (1,)), ((), ())), preferred_element_type=jnp.float32
    )


def gamma_rows_last(amplitude, owned_all):
    width = amplitude.shape[0]
    rows = owned_all.shape[0]
    out = pl.pallas_call(
        gamma_kernel,
        out_shape=jax.ShapeDtypeStruct((width, 1, rows), jnp.float32),
        in_specs=[pl.BlockSpec(memory_space=pltpu.VMEM)] * 2,
        out_specs=pl.BlockSpec(memory_space=pltpu.VMEM),
        compiler_params=pltpu.CompilerParams(vmem_limit_bytes=48 * 2**20),
    )(amplitude, owned_all)
    return out.transpose(1, 2, 0)


def body(b_aux, occ_energies, vir_energies, owners, *, shards, n_aux, by_partials):
    local = b_aux[0]
    width = local.shape[1] // shards
    col_energy = (vir_energies[None, :] - occ_energies[:, None]).reshape(-1)
    shard_index = lax.axis_index(COLS)
    energy_mine = lax.dynamic_slice_in_dim(col_energy, shard_index * width, width, 0)
    owned, owner_energy = owner_columns(local, col_energy, owners, width)
    owned_all = lax.all_gather(owned, COLS, axis=0, tiled=True)
    if by_partials:
        coupling = coupling_by_partials(local, owned, shards, width)
    else:
        coupling = coupling_by_columns(local, owned_all, shards, width)
    coupling = exchange_sum(coupling, "aux", n_aux)
    denominator = energy_mine[:, None] + owner_energy[None, :]
    amplitude = (os_scale * coupling / denominator).astype(jnp.bfloat16)
    return gamma_rows_last(amplitude, owned_all)


def solution(mesh):
    shards = mesh.shape["col"] * mesh.shape["rep"]

    def run(b_aux, occ_energies, vir_energies, owners):
        ncol = b_aux.shape[2]
        partial_bytes = ncol * owners.shape[0] * (ncol // shards) * 4
        by_partials = partial_bytes <= PARTIAL_BYTES_MAX
        placed = (P(("groups", "aux"), COLS, None), P("groups"), P("groups"), P())
        return jax.shard_map(
            lambda *a: body(*a, shards=shards, n_aux=mesh.shape["aux"], by_partials=by_partials),
            mesh=mesh,
            in_specs=placed,
            out_specs=P(("groups", "aux"), None, COLS),
            check_vma=False,
        )(b_aux, occ_energies, vir_energies, owners)

    return run
```

```python
import jax
import jax.numpy as jnp
from jax import lax
from jax.experimental import pallas as pl
from jax.experimental.pallas import tpu as pltpu
from jax.sharding import PartitionSpec as P

os_scale = 1.3
COLS = ("col", "rep")
PARTIAL_BYTES_MAX = 0
LANES = 128


def owner_columns(local, col_energy, owners, width):
    owned = []
    owner_energy = []
    for step_index in range(owners.shape[0]):
        first = owners[step_index] * width
        owned.append(lax.dynamic_slice_in_dim(local, first, width, 1))
        owner_energy.append(lax.dynamic_slice_in_dim(col_energy, first, width, 0))
    return jnp.concatenate(owned, axis=1), jnp.concatenate(owner_energy, axis=0)


def coupling_by_partials(local, owned, shards, width):
    rows = local.shape[0]
    blocked = local.reshape(rows, shards, width)
    partial_value = lax.dot_general(
        blocked, owned, (((0,), (0,)), ((), ())), preferred_element_type=jnp.float32
    )
    return lax.psum_scatter(partial_value, COLS, scatter_dimension=0, tiled=False)


def coupling_by_columns(local, owned_all, shards, width, n_aux):
    rows = local.shape[0]
    blocked = local.reshape(rows, shards, width).transpose(1, 0, 2)
    edges = sorted(set([0, min(LANES, width), width]))
    pieces = {}
    previous = None
    for first, last in list(zip(edges[:-1], edges[1:]))[::-1]:
        chunk = blocked[:, :, first:last]
        if previous is not None:
            chunk, _ = lax.optimization_barrier((chunk, previous))
        moved = lax.all_to_all(chunk, COLS, split_axis=0, concat_axis=0, tiled=True)
        piece = lax.dot_general(
            moved.reshape(shards * rows, last - first), owned_all, (((0,), (0,)), ((), ())),
            preferred_element_type=jnp.float32,
        )
        previous = piece
        pieces[first] = exchange_sum(piece, "aux", n_aux)
    return jnp.concatenate([pieces[first] for first in sorted(pieces)], axis=0)


def exchange_sum(value, axis, size):
    total = value
    for step in range(1, size):
        total = total + lax.ppermute(value, axis, [(i, (i + step) % size) for i in range(size)])
    return total


def gamma_kernel(amp_ref, owned_ref, out_ref):
    out_ref[:, 0, :] = lax.dot_general(
        amp_ref[...], owned_ref[...], (((1,), (1,)), ((), ())), preferred_element_type=jnp.float32
    )


def gamma_rows_last(amplitude, owned_all):
    width = amplitude.shape[0]
    rows = owned_all.shape[0]
    out = pl.pallas_call(
        gamma_kernel,
        out_shape=jax.ShapeDtypeStruct((width, 1, rows), jnp.float32),
        in_specs=[pl.BlockSpec(memory_space=pltpu.VMEM)] * 2,
        out_specs=pl.BlockSpec(memory_space=pltpu.VMEM),
        compiler_params=pltpu.CompilerParams(vmem_limit_bytes=48 * 2**20),
    )(amplitude, owned_all)
    return out.transpose(1, 2, 0)


def body(b_aux, occ_energies, vir_energies, owners, *, shards, n_aux, by_partials):
    local = b_aux[0]
    width = local.shape[1] // shards
    col_energy = (vir_energies[None, :] - occ_energies[:, None]).reshape(-1)
    shard_index = lax.axis_index(COLS)
    energy_mine = lax.dynamic_slice_in_dim(col_energy, shard_index * width, width, 0)
    owned, owner_energy = owner_columns(local, col_energy, owners, width)
    owned_all = lax.all_gather(owned, COLS, axis=0, tiled=True)
    if by_partials:
        coupling = coupling_by_partials(local, owned, shards, width)
        coupling = exchange_sum(coupling, "aux", n_aux)
    else:
        coupling = coupling_by_columns(local, owned_all, shards, width, n_aux)
    denominator = energy_mine[:, None] + owner_energy[None, :]
    amplitude = (os_scale * coupling / denominator).astype(jnp.bfloat16)
    return gamma_rows_last(amplitude, owned_all)


def solution(mesh):
    shards = mesh.shape["col"] * mesh.shape["rep"]

    def run(b_aux, occ_energies, vir_energies, owners):
        ncol = b_aux.shape[2]
        partial_bytes = ncol * owners.shape[0] * (ncol // shards) * 4
        by_partials = partial_bytes <= PARTIAL_BYTES_MAX
        placed = (P(("groups", "aux"), COLS, None), P("groups"), P("groups"), P())
        return jax.shard_map(
            lambda *a: body(*a, shards=shards, n_aux=mesh.shape["aux"], by_partials=by_partials),
            mesh=mesh,
            in_specs=placed,
            out_specs=P(("groups", "aux"), None, COLS),
            check_vma=False,
        )(b_aux, occ_energies, vir_energies, owners)

    return run
```

```python
import functools

import jax
import jax.numpy as jnp
from jax import lax
from jax.experimental import pallas as pl
from jax.experimental.pallas import tpu as pltpu
from jax.experimental.layout import Layout, with_layout_constraint
from jax.sharding import PartitionSpec as P

os_scale = 1.3
COLS = ("col", "rep")
PARTIAL_BYTES_MAX = 0
LINE_MAX = 8


def owner_columns(local, col_energy, owners, width):
    owned = []
    owner_energy = []
    for step_index in range(owners.shape[0]):
        first = owners[step_index] * width
        owned.append(lax.dynamic_slice_in_dim(local, first, width, 1))
        owner_energy.append(lax.dynamic_slice_in_dim(col_energy, first, width, 0))
    return jnp.concatenate(owned, axis=1), jnp.concatenate(owner_energy, axis=0)


def coupling_by_partials(local, owned, shards, width):
    rows = local.shape[0]
    blocked = local.reshape(rows, shards, width)
    partial_value = lax.dot_general(
        blocked, owned, (((0,), (0,)), ((), ())), preferred_element_type=jnp.float32
    )
    return lax.psum_scatter(partial_value, COLS, scatter_dimension=0, tiled=False)


def move_columns(local, shards, width):
    rows = local.shape[0]
    blocked = local.reshape(rows, shards, width).transpose(1, 0, 2)
    return lax.all_to_all(blocked, COLS, split_axis=0, concat_axis=0, tiled=True)


def coupling_by_columns(moved, owned_blocks, n_col, n_rep, width, by_chip):
    rows = moved.shape[1]
    shards = n_col * n_rep
    if by_chip:
        moved = moved.reshape(n_col, n_rep, rows, width).transpose(1, 0, 2, 3)
    return lax.dot_general(
        moved.reshape(shards * rows, width),
        owned_blocks.reshape(shards * rows, owned_blocks.shape[-1]),
        (((0,), (0,)), ((), ())),
        preferred_element_type=jnp.float32,
    )


def exchange_sum(value, axis, size):
    total = value
    for step in range(1, size):
        total = total + lax.ppermute(value, axis, [(i, (i + step) % size) for i in range(size)])
    return total


def gamma_kernel(amp_ref, owned_ref, out_ref, *, order):
    outer, inner, rows = owned_ref.shape[:3]
    for a in range(outer):
        for b in range(inner):
            start = order(a, b) * rows
            out_ref[:, 0, start : start + rows] = lax.dot_general(
                amp_ref[...], owned_ref[a, b], (((1,), (1,)), ((), ())),
                preferred_element_type=jnp.float32,
            )


def gamma_rows_last(amplitude, owned_blocks, order):
    width = amplitude.shape[0]
    rows = owned_blocks.shape[0] * owned_blocks.shape[1] * owned_blocks.shape[2]
    out = pl.pallas_call(
        functools.partial(gamma_kernel, order=order),
        out_shape=jax.ShapeDtypeStruct((width, 1, rows), jnp.float32),
        in_specs=[pl.BlockSpec(memory_space=pltpu.VMEM)] * 2,
        out_specs=pl.BlockSpec(memory_space=pltpu.VMEM),
        compiler_params=pltpu.CompilerParams(vmem_limit_bytes=48 * 2**20),
    )(amplitude, owned_blocks)
    return out.transpose(1, 2, 0)


def gather_by_chip(owned, after):
    owned = with_layout_constraint(owned, Layout((0, 1)))
    gathered = lax.all_gather(owned, "col", axis=0, tiled=False)
    gathered, _ = lax.optimization_barrier((gathered, after))
    return lax.all_gather(gathered, "rep", axis=0, tiled=False)


def body(b_aux, occ_energies, vir_energies, owners, *, n_col, n_rep, n_aux, by_partials):
    shards = n_col * n_rep
    local = b_aux[0]
    width = local.shape[1] // shards
    col_energy = (vir_energies[None, :] - occ_energies[:, None]).reshape(-1)
    shard_index = lax.axis_index(COLS)
    energy_mine = lax.dynamic_slice_in_dim(col_energy, shard_index * width, width, 0)
    owned, owner_energy = owner_columns(local, col_energy, owners, width)
    by_chip = n_col <= LINE_MAX and not by_partials
    moved = None if by_partials else move_columns(local, shards, width)
    if by_chip:
        owned_blocks = gather_by_chip(owned, moved)
        order = lambda a, b: b * n_rep + a
    else:
        owned_blocks = lax.all_gather(owned, COLS, axis=0, tiled=True)[None, None]
        order = lambda a, b: 0
    if by_partials:
        coupling = coupling_by_partials(local, owned, shards, width)
    else:
        coupling = coupling_by_columns(moved, owned_blocks, n_col, n_rep, width, by_chip)
    coupling = exchange_sum(coupling, "aux", n_aux)
    denominator = energy_mine[:, None] + owner_energy[None, :]
    amplitude = (os_scale * coupling / denominator).astype(jnp.bfloat16)
    return gamma_rows_last(amplitude, owned_blocks, order)


def solution(mesh):
    n_col, n_rep = mesh.shape["col"], mesh.shape["rep"]
    shards = n_col * n_rep

    def run(b_aux, occ_energies, vir_energies, owners):
        ncol = b_aux.shape[2]
        partial_bytes = ncol * owners.shape[0] * (ncol // shards) * 4
        by_partials = partial_bytes <= PARTIAL_BYTES_MAX
        placed = (P(("groups", "aux"), COLS, None), P("groups"), P("groups"), P())
        return jax.shard_map(
            lambda *a: body(*a, n_col=n_col, n_rep=n_rep, n_aux=mesh.shape["aux"], by_partials=by_partials),
            mesh=mesh,
            in_specs=placed,
            out_specs=P(("groups", "aux"), None, COLS),
            check_vma=False,
        )(b_aux, occ_energies, vir_energies, owners)

    return run
```

```python
import jax
import jax.numpy as jnp
from jax import lax
from jax.experimental import pallas as pl
from jax.experimental.pallas import tpu as pltpu
from jax.sharding import PartitionSpec as P

os_scale = 1.3
COLS = ("col", "rep")
PARTIAL_BYTES_MAX = 0
LANES = 128


def owner_columns(local, col_energy, owners, width):
    owned = []
    owner_energy = []
    for step_index in range(owners.shape[0]):
        first = owners[step_index] * width
        owned.append(lax.dynamic_slice_in_dim(local, first, width, 1))
        owner_energy.append(lax.dynamic_slice_in_dim(col_energy, first, width, 0))
    return jnp.concatenate(owned, axis=1), jnp.concatenate(owner_energy, axis=0)


def coupling_by_partials(local, owned, shards, width):
    rows = local.shape[0]
    blocked = local.reshape(rows, shards, width)
    partial_value = lax.dot_general(
        blocked, owned, (((0,), (0,)), ((), ())), preferred_element_type=jnp.float32
    )
    return lax.psum_scatter(partial_value, COLS, scatter_dimension=0, tiled=False)


def coupling_by_columns(local, owned_all, shards, width, n_aux):
    rows = local.shape[0]
    blocked = local.reshape(rows, shards, width).transpose(1, 0, 2)
    split = (width // LANES) * LANES
    edges = [0, split, width] if 0 < split < width else [0, width]
    pieces = []
    previous = None
    for first, last in zip(edges[:-1], edges[1:]):
        chunk = blocked[:, :, first:last]
        if previous is not None:
            chunk, _ = lax.optimization_barrier((chunk, previous))
        moved = lax.all_to_all(chunk, COLS, split_axis=0, concat_axis=0, tiled=True)
        previous = lax.dot_general(
            moved.reshape(shards * rows, last - first), owned_all, (((0,), (0,)), ((), ())),
            preferred_element_type=jnp.float32,
        )
        pieces.append(exchange_sum(previous, "aux", n_aux))
    return jnp.concatenate(pieces, axis=0)


def exchange_sum(value, axis, size):
    total = value
    for step in range(1, size):
        total = total + lax.ppermute(value, axis, [(i, (i + step) % size) for i in range(size)])
    return total


def gamma_kernel(amp_ref, owned_ref, out_ref):
    out_ref[:, 0, :] = lax.dot_general(
        amp_ref[...], owned_ref[...], (((1,), (1,)), ((), ())), preferred_element_type=jnp.float32
    )


def gamma_rows_last(amplitude, owned_all):
    width = amplitude.shape[0]
    rows = owned_all.shape[0]
    out = pl.pallas_call(
        gamma_kernel,
        out_shape=jax.ShapeDtypeStruct((width, 1, rows), jnp.float32),
        in_specs=[pl.BlockSpec(memory_space=pltpu.VMEM)] * 2,
        out_specs=pl.BlockSpec(memory_space=pltpu.VMEM),
        compiler_params=pltpu.CompilerParams(vmem_limit_bytes=48 * 2**20),
    )(amplitude, owned_all)
    return out.transpose(1, 2, 0)


def body(b_aux, occ_energies, vir_energies, owners, *, shards, n_aux, by_partials):
    local = b_aux[0]
    width = local.shape[1] // shards
    col_energy = (vir_energies[None, :] - occ_energies[:, None]).reshape(-1)
    shard_index = lax.axis_index(COLS)
    energy_mine = lax.dynamic_slice_in_dim(col_energy, shard_index * width, width, 0)
    owned, owner_energy = owner_columns(local, col_energy, owners, width)
    owned_all = lax.all_gather(owned, COLS, axis=0, tiled=True)
    if by_partials:
        coupling = coupling_by_partials(local, owned, shards, width)
        coupling = exchange_sum(coupling, "aux", n_aux)
    else:
        coupling = coupling_by_columns(local, owned_all, shards, width, n_aux)
    denominator = energy_mine[:, None] + owner_energy[None, :]
    amplitude = (os_scale * coupling / denominator).astype(jnp.bfloat16)
    return gamma_rows_last(amplitude, owned_all)


def solution(mesh):
    shards = mesh.shape["col"] * mesh.shape["rep"]

    def run(b_aux, occ_energies, vir_energies, owners):
        ncol = b_aux.shape[2]
        partial_bytes = ncol * owners.shape[0] * (ncol // shards) * 4
        by_partials = partial_bytes <= PARTIAL_BYTES_MAX
        placed = (P(("groups", "aux"), COLS, None), P("groups"), P("groups"), P())
        return jax.shard_map(
            lambda *a: body(*a, shards=shards, n_aux=mesh.shape["aux"], by_partials=by_partials),
            mesh=mesh,
            in_specs=placed,
            out_specs=P(("groups", "aux"), None, COLS),
            check_vma=False,
        )(b_aux, occ_energies, vir_energies, owners)

    return run
```

```python
import jax
import jax.numpy as jnp
from jax import lax
from jax.experimental import pallas as pl
from jax.experimental.pallas import tpu as pltpu
from jax.sharding import PartitionSpec as P

os_scale = 1.3
COLS = ("col", "rep")
PARTIAL_BYTES_MAX = 0
LANES = 128
ROW_BLOCK = 1024


def owner_columns(local, col_energy, owners, width):
    owned = []
    owner_energy = []
    for step_index in range(owners.shape[0]):
        first = owners[step_index] * width
        owned.append(lax.dynamic_slice_in_dim(local, first, width, 1))
        owner_energy.append(lax.dynamic_slice_in_dim(col_energy, first, width, 0))
    return jnp.concatenate(owned, axis=1), jnp.concatenate(owner_energy, axis=0)


def coupling_by_partials(local, owned, shards, width):
    rows = local.shape[0]
    blocked = local.reshape(rows, shards, width)
    partial_value = lax.dot_general(
        blocked, owned, (((0,), (0,)), ((), ())), preferred_element_type=jnp.float32
    )
    return lax.psum_scatter(partial_value, COLS, scatter_dimension=0, tiled=False)


def coupling_by_columns(local, owned_all, shards, width, n_aux):
    rows = local.shape[0]
    blocked = local.reshape(rows, shards, width).transpose(1, 0, 2)
    split = (width // LANES) * LANES
    edges = [0, split, width] if 0 < split < width else [0, width]
    pieces = []
    previous = None
    for first, last in zip(edges[:-1], edges[1:]):
        chunk = blocked[:, :, first:last]
        if previous is not None:
            chunk, _ = lax.optimization_barrier((chunk, previous))
        moved = lax.all_to_all(chunk, COLS, split_axis=0, concat_axis=0, tiled=True)
        previous = lax.dot_general(
            moved.reshape(shards * rows, last - first), owned_all, (((0,), (0,)), ((), ())),
            preferred_element_type=jnp.float32,
        )
        pieces.append(exchange_sum(previous, "aux", n_aux))
    return jnp.concatenate(pieces, axis=0)


def exchange_sum(value, axis, size):
    total = value
    for step in range(1, size):
        total = total + lax.ppermute(value, axis, [(i, (i + step) % size) for i in range(size)])
    return total


def gamma_kernel(amp_ref, owned_ref, out_ref):
    out_ref[:, 0, :] = lax.dot_general(
        amp_ref[...], owned_ref[...], (((1,), (1,)), ((), ())), preferred_element_type=jnp.float32
    )


def gamma_rows_last(amplitude, owned_all):
    width, depth = amplitude.shape
    rows = owned_all.shape[0]
    block = ROW_BLOCK if rows % ROW_BLOCK == 0 else rows
    out = pl.pallas_call(
        gamma_kernel,
        out_shape=jax.ShapeDtypeStruct((width, 1, rows), jnp.float32),
        grid=(rows // block,),
        in_specs=[
            pl.BlockSpec((width, depth), lambda i: (0, 0)),
            pl.BlockSpec((block, depth), lambda i: (i, 0)),
        ],
        out_specs=pl.BlockSpec((width, 1, block), lambda i: (0, 0, i)),
    )(amplitude, owned_all)
    return out.transpose(1, 2, 0)


def body(b_aux, occ_energies, vir_energies, owners, *, shards, n_aux, by_partials):
    local = b_aux[0]
    width = local.shape[1] // shards
    col_energy = (vir_energies[None, :] - occ_energies[:, None]).reshape(-1)
    shard_index = lax.axis_index(COLS)
    energy_mine = lax.dynamic_slice_in_dim(col_energy, shard_index * width, width, 0)
    owned, owner_energy = owner_columns(local, col_energy, owners, width)
    owned_all = lax.all_gather(owned, COLS, axis=0, tiled=True)
    if by_partials:
        coupling = coupling_by_partials(local, owned, shards, width)
        coupling = exchange_sum(coupling, "aux", n_aux)
    else:
        coupling = coupling_by_columns(local, owned_all, shards, width, n_aux)
    denominator = energy_mine[:, None] + owner_energy[None, :]
    amplitude = (os_scale * coupling / denominator).astype(jnp.bfloat16)
    return gamma_rows_last(amplitude, owned_all)


def solution(mesh):
    shards = mesh.shape["col"] * mesh.shape["rep"]

    def run(b_aux, occ_energies, vir_energies, owners):
        ncol = b_aux.shape[2]
        partial_bytes = ncol * owners.shape[0] * (ncol // shards) * 4
        by_partials = partial_bytes <= PARTIAL_BYTES_MAX
        placed = (P(("groups", "aux"), COLS, None), P("groups"), P("groups"), P())
        return jax.shard_map(
            lambda *a: body(*a, shards=shards, n_aux=mesh.shape["aux"], by_partials=by_partials),
            mesh=mesh,
            in_specs=placed,
            out_specs=P(("groups", "aux"), None, COLS),
            check_vma=False,
        )(b_aux, occ_energies, vir_energies, owners)

    return run
```

```python
import jax
import jax.numpy as jnp
from jax import lax
from jax.experimental import pallas as pl
from jax.experimental.pallas import tpu as pltpu
from jax.experimental.layout import Layout, with_layout_constraint
from jax.sharding import PartitionSpec as P

os_scale = 1.3
COLS = ("col", "rep")
PARTIAL_BYTES_MAX = 16 * 2**20
LANES = 128
ROW_BLOCK = 1024


def owner_columns(local, col_energy, owners, width):
    owned = []
    owner_energy = []
    for step_index in range(owners.shape[0]):
        first = owners[step_index] * width
        owned.append(lax.dynamic_slice_in_dim(local, first, width, 1))
        owner_energy.append(lax.dynamic_slice_in_dim(col_energy, first, width, 0))
    return jnp.concatenate(owned, axis=1), jnp.concatenate(owner_energy, axis=0)


def coupling_by_partials(local, owned, shards, width):
    rows = local.shape[0]
    blocked = local.reshape(rows, shards, width)
    partial_value = lax.dot_general(
        blocked, owned, (((0,), (0,)), ((), ())), preferred_element_type=jnp.float32
    )
    return lax.psum_scatter(partial_value, COLS, scatter_dimension=0, tiled=False)


def coupling_by_columns(local, owned_all, shards, width, n_aux):
    rows = local.shape[0]
    blocked = local.reshape(rows, shards, width).transpose(1, 0, 2)
    split = (width // LANES) * LANES
    edges = [0, split, width] if 0 < split < width else [0, width]
    pieces = []
    previous = None
    for first, last in zip(edges[:-1], edges[1:]):
        chunk = blocked[:, :, first:last]
        if previous is not None:
            chunk, _ = lax.optimization_barrier((chunk, previous))
        moved = lax.all_to_all(chunk, COLS, split_axis=0, concat_axis=0, tiled=True)
        previous = lax.dot_general(
            moved.reshape(shards * rows, last - first), owned_all, (((0,), (0,)), ((), ())),
            preferred_element_type=jnp.float32,
        )
        pieces.append(exchange_sum(previous, "aux", n_aux))
    return jnp.concatenate(pieces, axis=0)


def exchange_sum(value, axis, size):
    total = value
    for step in range(1, size):
        total = total + lax.ppermute(value, axis, [(i, (i + step) % size) for i in range(size)])
    return total


def gamma_kernel(amp_ref, owned_ref, out_ref):
    out_ref[:, 0, :] = lax.dot_general(
        amp_ref[...], owned_ref[...], (((1,), (1,)), ((), ())), preferred_element_type=jnp.float32
    )


def gamma_rows_last(amplitude, owned_all, block=None, place=None):
    width, depth = amplitude.shape
    rows = owned_all.shape[0]
    if block is None:
        block = ROW_BLOCK if rows % ROW_BLOCK == 0 else rows
        place = lambda i: i
    out = pl.pallas_call(
        gamma_kernel,
        out_shape=jax.ShapeDtypeStruct((width, 1, rows), jnp.float32),
        grid=(rows // block,),
        in_specs=[
            pl.BlockSpec((width, depth), lambda i: (0, 0)),
            pl.BlockSpec((block, depth), lambda i: (i, 0)),
        ],
        out_specs=pl.BlockSpec((width, 1, block), lambda i: (0, 0, place(i))),
    )(amplitude, owned_all)
    return out.transpose(1, 2, 0)


def gather_by_chip(owned):
    owned = with_layout_constraint(owned, Layout((0, 1)))
    gathered = lax.all_gather(owned, "col", axis=0, tiled=True)
    return lax.all_gather(gathered, "rep", axis=0, tiled=True)


def body(b_aux, occ_energies, vir_energies, owners, *, shards, n_rep, n_aux, by_partials):
    local = b_aux[0]
    width = local.shape[1] // shards
    col_energy = (vir_energies[None, :] - occ_energies[:, None]).reshape(-1)
    shard_index = lax.axis_index(COLS)
    energy_mine = lax.dynamic_slice_in_dim(col_energy, shard_index * width, width, 0)
    owned, owner_energy = owner_columns(local, col_energy, owners, width)
    if by_partials:
        n_col = shards // n_rep
        owned_all = gather_by_chip(owned)
        block = local.shape[0]
        place = lambda i: (i % n_col) * n_rep + i // n_col
    else:
        owned_all = lax.all_gather(owned, COLS, axis=0, tiled=True)
        block = place = None
    if by_partials:
        coupling = coupling_by_partials(local, owned, shards, width)
        coupling = exchange_sum(coupling, "aux", n_aux)
    else:
        coupling = coupling_by_columns(local, owned_all, shards, width, n_aux)
    denominator = energy_mine[:, None] + owner_energy[None, :]
    amplitude = (os_scale * coupling / denominator).astype(jnp.bfloat16)
    return gamma_rows_last(amplitude, owned_all, block, place)


def solution(mesh):
    shards = mesh.shape["col"] * mesh.shape["rep"]

    def run(b_aux, occ_energies, vir_energies, owners):
        ncol = b_aux.shape[2]
        partial_bytes = ncol * owners.shape[0] * (ncol // shards) * 4
        by_partials = partial_bytes <= PARTIAL_BYTES_MAX
        placed = (P(("groups", "aux"), COLS, None), P("groups"), P("groups"), P())
        return jax.shard_map(
            lambda *a: body(
                *a, shards=shards, n_rep=mesh.shape["rep"], n_aux=mesh.shape["aux"],
                by_partials=by_partials,
            ),
            mesh=mesh,
            in_specs=placed,
            out_specs=P(("groups", "aux"), None, COLS),
            check_vma=False,
        )(b_aux, occ_energies, vir_energies, owners)

    return run
```

```python
import jax
import jax.numpy as jnp
from jax import lax
from jax.experimental import pallas as pl
from jax.experimental.pallas import tpu as pltpu
from jax.sharding import PartitionSpec as P

os_scale = 1.3
COLS = ("col", "rep")
PARTIAL_BYTES_MAX = 0
LINE_MAX = 8


def owner_columns(local, col_energy, owners, width):
    owned = []
    owner_energy = []
    for step_index in range(owners.shape[0]):
        first = owners[step_index] * width
        owned.append(lax.dynamic_slice_in_dim(local, first, width, 1))
        owner_energy.append(lax.dynamic_slice_in_dim(col_energy, first, width, 0))
    return jnp.concatenate(owned, axis=1), jnp.concatenate(owner_energy, axis=0)


def coupling_by_partials(local, owned, shards, width):
    rows = local.shape[0]
    blocked = local.reshape(rows, shards, width)
    partial_value = lax.dot_general(
        blocked, owned, (((0,), (0,)), ((), ())), preferred_element_type=jnp.float32
    )
    return lax.psum_scatter(partial_value, COLS, scatter_dimension=0, tiled=False)


def coupling_by_columns(local, owned_all, shards, width, order=None):
    rows = local.shape[0]
    blocked = local.reshape(rows, shards, width).transpose(1, 0, 2)
    moved = lax.all_to_all(blocked, COLS, split_axis=0, concat_axis=0, tiled=True)
    if order is not None:
        moved = order(moved)
    return lax.dot_general(
        moved.reshape(shards * rows, width), owned_all, (((0,), (0,)), ((), ())),
        preferred_element_type=jnp.float32,
    )


def exchange_sum(value, axis, size):
    total = value
    for step in range(1, size):
        total = total + lax.ppermute(value, axis, [(i, (i + step) % size) for i in range(size)])
    return total


def gamma_kernel(ids_ref, amp_ref, owned_ref, out_ref):
    out_ref[:, 0, :] = lax.dot_general(
        amp_ref[...], owned_ref[...], (((1,), (1,)), ((), ())), preferred_element_type=jnp.float32
    )


def gamma_rows_last(amplitude, owned_all, ids, block, place):
    width, depth = amplitude.shape
    rows = owned_all.shape[0]
    out = pl.pallas_call(
        gamma_kernel,
        out_shape=jax.ShapeDtypeStruct((width, 1, rows), jnp.float32),
        grid_spec=pltpu.PrefetchScalarGridSpec(
            num_scalar_prefetch=1,
            grid=(rows // block,),
            in_specs=[
                pl.BlockSpec((width, depth), lambda i, ids: (0, 0)),
                pl.BlockSpec((block, depth), lambda i, ids: (i, 0)),
            ],
            out_specs=pl.BlockSpec((width, 1, block), lambda i, ids: (0, 0, place(i, ids))),
        ),
    )(ids, amplitude, owned_all)
    return out.transpose(1, 2, 0)


def gather_relative(owned, n_col, n_rep):
    mine = [owned]
    for step in range(1, n_col):
        mine.append(lax.ppermute(owned, "col", [(i, (i - step) % n_col) for i in range(n_col)]))
    mine = jnp.stack(mine)
    blocks = [mine]
    for step in range(1, n_rep):
        blocks.append(lax.ppermute(mine, "rep", [(i, (i - step) % n_rep) for i in range(n_rep)]))
    return jnp.stack(blocks, axis=1)


def relative_order(moved, n_col, n_rep):
    me = lax.axis_index("col")
    rep = lax.axis_index("rep")
    by_chip = moved.reshape((n_col, n_rep) + moved.shape[1:])
    doubled = jnp.concatenate([by_chip, by_chip], axis=0)
    by_chip = lax.dynamic_slice_in_dim(doubled, me, n_col, 0)
    doubled = jnp.concatenate([by_chip, by_chip], axis=1)
    return lax.dynamic_slice_in_dim(doubled, rep, n_rep, 1)


def body(b_aux, occ_energies, vir_energies, owners, *, shards, n_rep, n_aux, by_partials):
    local = b_aux[0]
    width = local.shape[1] // shards
    col_energy = (vir_energies[None, :] - occ_energies[:, None]).reshape(-1)
    shard_index = lax.axis_index(COLS)
    energy_mine = lax.dynamic_slice_in_dim(col_energy, shard_index * width, width, 0)
    owned, owner_energy = owner_columns(local, col_energy, owners, width)
    n_col = shards // n_rep
    rows = local.shape[0]
    ids = jnp.stack([lax.axis_index("col"), lax.axis_index("rep")]).astype(jnp.int32)
    if n_col <= LINE_MAX and not by_partials:
        owned_all = gather_relative(owned, n_col, n_rep).reshape(shards * rows, owned.shape[1])
        order = lambda moved: relative_order(moved, n_col, n_rep)
        block = rows
        place = lambda i, ids: ((ids[0] + i // n_rep) % n_col) * n_rep + (ids[1] + i % n_rep) % n_rep
    else:
        owned_all = lax.all_gather(owned, COLS, axis=0, tiled=True)
        order = None
        block = owned_all.shape[0]
        place = lambda i, ids: i
    if by_partials:
        coupling = coupling_by_partials(local, owned, shards, width)
    else:
        coupling = coupling_by_columns(local, owned_all, shards, width, order)
    coupling = exchange_sum(coupling, "aux", n_aux)
    denominator = energy_mine[:, None] + owner_energy[None, :]
    amplitude = (os_scale * coupling / denominator).astype(jnp.bfloat16)
    return gamma_rows_last(amplitude, owned_all, ids, block, place)


def solution(mesh):
    shards = mesh.shape["col"] * mesh.shape["rep"]

    def run(b_aux, occ_energies, vir_energies, owners):
        ncol = b_aux.shape[2]
        partial_bytes = ncol * owners.shape[0] * (ncol // shards) * 4
        by_partials = partial_bytes <= PARTIAL_BYTES_MAX
        placed = (P(("groups", "aux"), COLS, None), P("groups"), P("groups"), P())
        return jax.shard_map(
            lambda *a: body(
                *a, shards=shards, n_rep=mesh.shape["rep"], n_aux=mesh.shape["aux"],
                by_partials=by_partials,
            ),
            mesh=mesh,
            in_specs=placed,
            out_specs=P(("groups", "aux"), None, COLS),
            check_vma=False,
        )(b_aux, occ_energies, vir_energies, owners)

    return run
```

```python
import jax
import jax.numpy as jnp
from jax import lax
from jax.experimental import pallas as pl
from jax.experimental.pallas import tpu as pltpu
from jax.sharding import PartitionSpec as P

os_scale = 1.3
COLS = ("col", "rep")
PARTIAL_BYTES_MAX = 0
LINE_MAX = 8


def owner_columns(local, col_energy, owners, width):
    owned = []
    owner_energy = []
    for step_index in range(owners.shape[0]):
        first = owners[step_index] * width
        owned.append(lax.dynamic_slice_in_dim(local, first, width, 1))
        owner_energy.append(lax.dynamic_slice_in_dim(col_energy, first, width, 0))
    return jnp.concatenate(owned, axis=1), jnp.concatenate(owner_energy, axis=0)


def coupling_by_partials(local, owned, shards, width):
    rows = local.shape[0]
    blocked = local.reshape(rows, shards, width)
    partial_value = lax.dot_general(
        blocked, owned, (((0,), (0,)), ((), ())), preferred_element_type=jnp.float32
    )
    return lax.psum_scatter(partial_value, COLS, scatter_dimension=0, tiled=False)


def coupling_by_columns(local, owned_parts, shards, width, order=None):
    rows = local.shape[0]
    blocked = local.reshape(rows, shards, width).transpose(1, 0, 2)
    moved = lax.all_to_all(blocked, COLS, split_axis=0, concat_axis=0, tiled=True)
    moved_parts = [moved.reshape(shards * rows, width)] if order is None else order(moved)
    total = None
    for moved_part, owned_part in zip(moved_parts, owned_parts):
        term = lax.dot_general(
            moved_part, owned_part, (((0,), (0,)), ((), ())), preferred_element_type=jnp.float32
        )
        total = term if total is None else total + term
    return total


def exchange_sum(value, axis, size):
    total = value
    for step in range(1, size):
        total = total + lax.ppermute(value, axis, [(i, (i + step) % size) for i in range(size)])
    return total


def gamma_kernel(ids_ref, amp_ref, *refs):
    out_ref = refs[-1]
    owned_refs = refs[:-1]
    n_rep = len(owned_refs)
    rows = owned_refs[0].shape[0]
    for step, owned_ref in enumerate(owned_refs):
        start = pl.multiple_of(((ids_ref[1] + step) % n_rep) * rows, rows)
        out_ref[:, 0, pl.ds(start, rows)] = lax.dot_general(
            amp_ref[...], owned_ref[...], (((1,), (1,)), ((), ())),
            preferred_element_type=jnp.float32,
        )


def gamma_rows_last(amplitude, owned_parts, ids, block, place):
    width, depth = amplitude.shape
    n_parts = len(owned_parts)
    rows = owned_parts[0].shape[0] * n_parts
    out = pl.pallas_call(
        gamma_kernel,
        out_shape=jax.ShapeDtypeStruct((width, 1, rows), jnp.float32),
        grid_spec=pltpu.PrefetchScalarGridSpec(
            num_scalar_prefetch=1,
            grid=(rows // (block * n_parts),),
            in_specs=[pl.BlockSpec((width, depth), lambda i, ids: (0, 0))]
            + [pl.BlockSpec((block, depth), lambda i, ids: (i, 0))] * n_parts,
            out_specs=pl.BlockSpec(
                (width, 1, block * n_parts), lambda i, ids: (0, 0, place(i, ids))
            ),
        ),
    )(ids, amplitude, *owned_parts)
    return out.transpose(1, 2, 0)


def gather_relative(owned, n_col, n_rep):
    mine = [owned]
    for step in range(1, n_col):
        mine.append(lax.ppermute(owned, "col", [(i, (i - step) % n_col) for i in range(n_col)]))
    mine = jnp.concatenate(mine, axis=0)
    parts = [mine]
    for step in range(1, n_rep):
        parts.append(lax.ppermute(mine, "rep", [(i, (i - step) % n_rep) for i in range(n_rep)]))
    return parts


def relative_order(moved, n_col, n_rep):
    me = lax.axis_index("col")
    rep = lax.axis_index("rep")
    by_chip = moved.reshape((n_col, n_rep) + moved.shape[1:])
    doubled = jnp.concatenate([by_chip, by_chip], axis=0)
    by_chip = lax.dynamic_slice_in_dim(doubled, me, n_col, 0)
    parts = []
    for step in range(n_rep):
        part = lax.dynamic_index_in_dim(by_chip, (rep + step) % n_rep, 1, keepdims=False)
        parts.append(part.reshape((-1,) + moved.shape[2:]))
    return parts


def body(b_aux, occ_energies, vir_energies, owners, *, shards, n_rep, n_aux, by_partials):
    local = b_aux[0]
    width = local.shape[1] // shards
    col_energy = (vir_energies[None, :] - occ_energies[:, None]).reshape(-1)
    shard_index = lax.axis_index(COLS)
    energy_mine = lax.dynamic_slice_in_dim(col_energy, shard_index * width, width, 0)
    owned, owner_energy = owner_columns(local, col_energy, owners, width)
    n_col = shards // n_rep
    rows = local.shape[0]
    ids = jnp.stack([lax.axis_index("col"), lax.axis_index("rep")]).astype(jnp.int32)
    if n_col <= LINE_MAX and not by_partials:
        owned_parts = gather_relative(owned, n_col, n_rep)
        order = lambda moved: relative_order(moved, n_col, n_rep)
        block = rows
        place = lambda i, ids: (ids[0] + i) % n_col
    else:
        owned_parts = [lax.all_gather(owned, COLS, axis=0, tiled=True)]
        order = None
        block = owned_parts[0].shape[0]
        place = lambda i, ids: i
    if by_partials:
        coupling = coupling_by_partials(local, owned, shards, width)
    else:
        coupling = coupling_by_columns(local, owned_parts, shards, width, order)
    coupling = exchange_sum(coupling, "aux", n_aux)
    denominator = energy_mine[:, None] + owner_energy[None, :]
    amplitude = (os_scale * coupling / denominator).astype(jnp.bfloat16)
    return gamma_rows_last(amplitude, owned_parts, ids, block, place)


def solution(mesh):
    shards = mesh.shape["col"] * mesh.shape["rep"]

    def run(b_aux, occ_energies, vir_energies, owners):
        ncol = b_aux.shape[2]
        partial_bytes = ncol * owners.shape[0] * (ncol // shards) * 4
        by_partials = partial_bytes <= PARTIAL_BYTES_MAX
        placed = (P(("groups", "aux"), COLS, None), P("groups"), P("groups"), P())
        return jax.shard_map(
            lambda *a: body(
                *a, shards=shards, n_rep=mesh.shape["rep"], n_aux=mesh.shape["aux"],
                by_partials=by_partials,
            ),
            mesh=mesh,
            in_specs=placed,
            out_specs=P(("groups", "aux"), None, COLS),
            check_vma=False,
        )(b_aux, occ_energies, vir_energies, owners)

    return run
```

```python
import jax
import jax.numpy as jnp
from jax import lax
from jax.experimental import pallas as pl
from jax.experimental.pallas import tpu as pltpu
from jax.experimental.layout import Layout, with_layout_constraint
from jax.sharding import PartitionSpec as P

os_scale = 1.3
COLS = ("col", "rep")
PARTIAL_BYTES_MAX = 0
LINE_MAX = 8


def owner_columns(local, col_energy, owners, width):
    owned = []
    owner_energy = []
    for step_index in range(owners.shape[0]):
        first = owners[step_index] * width
        owned.append(lax.dynamic_slice_in_dim(local, first, width, 1))
        owner_energy.append(lax.dynamic_slice_in_dim(col_energy, first, width, 0))
    return jnp.concatenate(owned, axis=1), jnp.concatenate(owner_energy, axis=0)


def coupling_by_partials(local, owned, shards, width):
    rows = local.shape[0]
    blocked = local.reshape(rows, shards, width)
    partial_value = lax.dot_general(
        blocked, owned, (((0,), (0,)), ((), ())), preferred_element_type=jnp.float32
    )
    return lax.psum_scatter(partial_value, COLS, scatter_dimension=0, tiled=False)


def coupling_by_columns(local, owned_all, shards, width, order=None):
    rows = local.shape[0]
    blocked = local.reshape(rows, shards, width).transpose(1, 0, 2)
    moved = lax.all_to_all(blocked, COLS, split_axis=0, concat_axis=0, tiled=True)
    if order is not None:
        moved = order(moved)
    return lax.dot_general(
        moved.reshape(shards * rows, width), owned_all, (((0,), (0,)), ((), ())),
        preferred_element_type=jnp.float32,
    )


def exchange_sum(value, axis, size):
    total = value
    for step in range(1, size):
        total = total + lax.ppermute(value, axis, [(i, (i + step) % size) for i in range(size)])
    return total


def gamma_kernel(ids_ref, amp_ref, owned_ref, out_ref):
    out_ref[:, 0, :] = lax.dot_general(
        amp_ref[...], owned_ref[...], (((1,), (1,)), ((), ())), preferred_element_type=jnp.float32
    )


def gamma_rows_last(amplitude, owned_all, ids, block, place):
    width, depth = amplitude.shape
    rows = owned_all.shape[0]
    out = pl.pallas_call(
        gamma_kernel,
        out_shape=jax.ShapeDtypeStruct((width, 1, rows), jnp.float32),
        grid_spec=pltpu.PrefetchScalarGridSpec(
            num_scalar_prefetch=1,
            grid=(rows // block,),
            in_specs=[
                pl.BlockSpec((width, depth), lambda i, ids: (0, 0)),
                pl.BlockSpec((block, depth), lambda i, ids: (i, 0)),
            ],
            out_specs=pl.BlockSpec((width, 1, block), lambda i, ids: (0, 0, place(i, ids))),
        ),
    )(ids, amplitude, owned_all)
    return out.transpose(1, 2, 0)


def gather_relative(owned, n_col, n_rep):
    mine = [owned]
    for step in range(1, n_col):
        mine.append(lax.ppermute(owned, "col", [(i, (i - step) % n_col) for i in range(n_col)]))
    mine = jnp.stack(mine)
    blocks = [mine]
    for step in range(1, n_rep):
        blocks.append(lax.ppermute(mine, "rep", [(i, (i - step) % n_rep) for i in range(n_rep)]))
    stacked = jnp.stack(blocks, axis=1)
    return with_layout_constraint(stacked, Layout(tuple(range(stacked.ndim))))


def relative_order(moved, n_col, n_rep):
    me = lax.axis_index("col")
    rep = lax.axis_index("rep")
    by_chip = moved.reshape((n_col, n_rep) + moved.shape[1:])
    doubled = jnp.concatenate([by_chip, by_chip], axis=0)
    by_chip = lax.dynamic_slice_in_dim(doubled, me, n_col, 0)
    doubled = jnp.concatenate([by_chip, by_chip], axis=1)
    return lax.dynamic_slice_in_dim(doubled, rep, n_rep, 1)


def body(b_aux, occ_energies, vir_energies, owners, *, shards, n_rep, n_aux, by_partials):
    local = b_aux[0]
    width = local.shape[1] // shards
    col_energy = (vir_energies[None, :] - occ_energies[:, None]).reshape(-1)
    shard_index = lax.axis_index(COLS)
    energy_mine = lax.dynamic_slice_in_dim(col_energy, shard_index * width, width, 0)
    owned, owner_energy = owner_columns(local, col_energy, owners, width)
    n_col = shards // n_rep
    rows = local.shape[0]
    ids = jnp.stack([lax.axis_index("col"), lax.axis_index("rep")]).astype(jnp.int32)
    if n_col <= LINE_MAX and not by_partials:
        owned_all = gather_relative(owned, n_col, n_rep).reshape(shards * rows, owned.shape[1])
        order = lambda moved: relative_order(moved, n_col, n_rep)
        block = rows
        place = lambda i, ids: ((ids[0] + i // n_rep) % n_col) * n_rep + (ids[1] + i % n_rep) % n_rep
    else:
        owned_all = lax.all_gather(owned, COLS, axis=0, tiled=True)
        order = None
        block = owned_all.shape[0]
        place = lambda i, ids: i
    if by_partials:
        coupling = coupling_by_partials(local, owned, shards, width)
    else:
        coupling = coupling_by_columns(local, owned_all, shards, width, order)
    coupling = exchange_sum(coupling, "aux", n_aux)
    denominator = energy_mine[:, None] + owner_energy[None, :]
    amplitude = (os_scale * coupling / denominator).astype(jnp.bfloat16)
    return gamma_rows_last(amplitude, owned_all, ids, block, place)


def solution(mesh):
    shards = mesh.shape["col"] * mesh.shape["rep"]

    def run(b_aux, occ_energies, vir_energies, owners):
        ncol = b_aux.shape[2]
        partial_bytes = ncol * owners.shape[0] * (ncol // shards) * 4
        by_partials = partial_bytes <= PARTIAL_BYTES_MAX
        placed = (P(("groups", "aux"), COLS, None), P("groups"), P("groups"), P())
        return jax.shard_map(
            lambda *a: body(
                *a, shards=shards, n_rep=mesh.shape["rep"], n_aux=mesh.shape["aux"],
                by_partials=by_partials,
            ),
            mesh=mesh,
            in_specs=placed,
            out_specs=P(("groups", "aux"), None, COLS),
            check_vma=False,
        )(b_aux, occ_energies, vir_energies, owners)

    return run
```

```python
import functools

import jax
import jax.numpy as jnp
from jax import lax
from jax.experimental import pallas as pl
from jax.experimental.pallas import tpu as pltpu
from jax.sharding import PartitionSpec as P

os_scale = 1.3
COLS = ("col", "rep")
PARTIAL_BYTES_MAX = 0
LANES = 128


def owner_columns(local, col_energy, owners, width):
    owned = []
    owner_energy = []
    for step_index in range(owners.shape[0]):
        first = owners[step_index] * width
        owned.append(lax.dynamic_slice_in_dim(local, first, width, 1))
        owner_energy.append(lax.dynamic_slice_in_dim(col_energy, first, width, 0))
    return jnp.concatenate(owned, axis=1), jnp.concatenate(owner_energy, axis=0)


def coupling_by_partials(local, owned, shards, width):
    rows = local.shape[0]
    blocked = local.reshape(rows, shards, width)
    partial_value = lax.dot_general(
        blocked, owned, (((0,), (0,)), ((), ())), preferred_element_type=jnp.float32
    )
    return lax.psum_scatter(partial_value, COLS, scatter_dimension=0, tiled=False)


def coupling_by_columns(local, owned_all, shards, width, n_aux):
    rows = local.shape[0]
    blocked = local.reshape(rows, shards, width).transpose(1, 0, 2)
    split = (width // LANES) * LANES
    edges = [0, split, width] if 0 < split < width else [0, width]
    pieces = []
    previous = None
    for first, last in zip(edges[:-1], edges[1:]):
        chunk = blocked[:, :, first:last]
        if previous is not None:
            chunk, _ = lax.optimization_barrier((chunk, previous))
        moved = lax.all_to_all(chunk, COLS, split_axis=0, concat_axis=0, tiled=True)
        previous = lax.dot_general(
            moved.reshape(shards * rows, last - first), owned_all, (((0,), (0,)), ((), ())),
            preferred_element_type=jnp.float32,
        )
        pieces.append(exchange_sum(previous, "aux", n_aux))
    return pieces


def exchange_sum(value, axis, size):
    total = value
    for step in range(1, size):
        total = total + lax.ppermute(value, axis, [(i, (i + step) % size) for i in range(size)])
    return total


def gamma_kernel(amp_ref, owned_ref, out_ref):
    out_ref[:, 0, :] = lax.dot_general(
        amp_ref[...], owned_ref[...], (((1,), (1,)), ((), ())), preferred_element_type=jnp.float32
    )


def gamma_tail_kernel(amp_ref, owned_ref, prev_ref, out_ref, held, sem, *, first):
    held[:, 0, :] = lax.dot_general(
        amp_ref[...], owned_ref[...], (((1,), (1,)), ((), ())), preferred_element_type=jnp.float32
    )
    copy = pltpu.make_async_copy(held, out_ref.at[pl.ds(first, held.shape[0])], sem)
    copy.start()
    copy.wait()


def gamma_rows_last(amp_pieces, owned_all, width):
    rows = owned_all.shape[0]
    head = amp_pieces[0].shape[0]
    depth = owned_all.shape[1]
    out = pl.pallas_call(
        gamma_kernel,
        out_shape=jax.ShapeDtypeStruct((width, 1, rows), jnp.float32),
        grid=(1,),
        in_specs=[
            pl.BlockSpec((head, depth), lambda i: (0, 0)),
            pl.BlockSpec((rows, depth), lambda i: (0, 0)),
        ],
        out_specs=pl.BlockSpec((head, 1, rows), lambda i: (0, 0, 0)),
        compiler_params=pltpu.CompilerParams(vmem_limit_bytes=48 * 2**20),
    )(amp_pieces[0], owned_all)
    if len(amp_pieces) > 1:
        tail = amp_pieces[1].shape[0]
        out = pl.pallas_call(
            functools.partial(gamma_tail_kernel, first=head),
            out_shape=jax.ShapeDtypeStruct((width, 1, rows), jnp.float32),
            in_specs=[pl.BlockSpec(memory_space=pltpu.VMEM)] * 2
            + [pl.BlockSpec(memory_space=pl.ANY)],
            out_specs=pl.BlockSpec(memory_space=pl.ANY),
            scratch_shapes=[pltpu.VMEM((tail, 1, rows), jnp.float32), pltpu.SemaphoreType.DMA],
            input_output_aliases={2: 0},
            compiler_params=pltpu.CompilerParams(vmem_limit_bytes=48 * 2**20),
        )(amp_pieces[1], owned_all, out)
    return out.transpose(1, 2, 0)


def body(b_aux, occ_energies, vir_energies, owners, *, shards, n_aux, by_partials):
    local = b_aux[0]
    width = local.shape[1] // shards
    col_energy = (vir_energies[None, :] - occ_energies[:, None]).reshape(-1)
    shard_index = lax.axis_index(COLS)
    energy_mine = lax.dynamic_slice_in_dim(col_energy, shard_index * width, width, 0)
    owned, owner_energy = owner_columns(local, col_energy, owners, width)
    owned_all = lax.all_gather(owned, COLS, axis=0, tiled=True)
    if by_partials:
        coupling = coupling_by_partials(local, owned, shards, width)
        pieces = [exchange_sum(coupling, "aux", n_aux)]
    else:
        pieces = coupling_by_columns(local, owned_all, shards, width, n_aux)
    amp_pieces = []
    first = 0
    for piece in pieces:
        last = first + piece.shape[0]
        denominator = energy_mine[first:last, None] + owner_energy[None, :]
        amp_pieces.append((os_scale * piece / denominator).astype(jnp.bfloat16))
        first = last
    return gamma_rows_last(amp_pieces, owned_all, width)


def solution(mesh):
    shards = mesh.shape["col"] * mesh.shape["rep"]

    def run(b_aux, occ_energies, vir_energies, owners):
        ncol = b_aux.shape[2]
        partial_bytes = ncol * owners.shape[0] * (ncol // shards) * 4
        by_partials = partial_bytes <= PARTIAL_BYTES_MAX
        placed = (P(("groups", "aux"), COLS, None), P("groups"), P("groups"), P())
        return jax.shard_map(
            lambda *a: body(*a, shards=shards, n_aux=mesh.shape["aux"], by_partials=by_partials),
            mesh=mesh,
            in_specs=placed,
            out_specs=P(("groups", "aux"), None, COLS),
            check_vma=False,
        )(b_aux, occ_energies, vir_energies, owners)

    return run
```

```python
import jax
import jax.numpy as jnp
from jax import lax
from jax.experimental import pallas as pl
from jax.experimental.pallas import tpu as pltpu
from jax.sharding import PartitionSpec as P

os_scale = 1.3
COLS = ("col", "rep")
PARTIAL_BYTES_MAX = 0
LANES = 128
ROW_BLOCK = 2048


def owner_columns(local, col_energy, owners, width):
    owned = []
    owner_energy = []
    for step_index in range(owners.shape[0]):
        first = owners[step_index] * width
        owned.append(lax.dynamic_slice_in_dim(local, first, width, 1))
        owner_energy.append(lax.dynamic_slice_in_dim(col_energy, first, width, 0))
    return jnp.concatenate(owned, axis=1), jnp.concatenate(owner_energy, axis=0)


def coupling_by_partials(local, owned, shards, width):
    rows = local.shape[0]
    blocked = local.reshape(rows, shards, width)
    partial_value = lax.dot_general(
        blocked, owned, (((0,), (0,)), ((), ())), preferred_element_type=jnp.float32
    )
    return lax.psum_scatter(partial_value, COLS, scatter_dimension=0, tiled=False)


def coupling_by_columns(local, owned_all, shards, width, n_aux):
    rows = local.shape[0]
    blocked = local.reshape(rows, shards, width).transpose(1, 0, 2)
    split = (width // LANES) * LANES
    edges = [0, split, width] if 0 < split < width else [0, width]
    pieces = []
    previous = None
    for first, last in zip(edges[:-1], edges[1:]):
        chunk = blocked[:, :, first:last]
        if previous is not None:
            chunk, _ = lax.optimization_barrier((chunk, previous))
        moved = lax.all_to_all(chunk, COLS, split_axis=0, concat_axis=0, tiled=True)
        previous = lax.dot_general(
            moved.reshape(shards * rows, last - first), owned_all, (((0,), (0,)), ((), ())),
            preferred_element_type=jnp.float32,
        )
        pieces.append(exchange_sum(previous, "aux", n_aux))
    return jnp.concatenate(pieces, axis=0)


def exchange_sum(value, axis, size):
    total = value
    for step in range(1, size):
        total = total + lax.ppermute(value, axis, [(i, (i + step) % size) for i in range(size)])
    return total


def gamma_kernel(amp_ref, owned_ref, out_ref):
    out_ref[:, 0, :] = lax.dot_general(
        amp_ref[...], owned_ref[...], (((1,), (1,)), ((), ())), preferred_element_type=jnp.float32
    )


def gamma_rows_last(amplitude, owned_all):
    width, depth = amplitude.shape
    rows = owned_all.shape[0]
    block = ROW_BLOCK if rows % ROW_BLOCK == 0 else rows
    out = pl.pallas_call(
        gamma_kernel,
        out_shape=jax.ShapeDtypeStruct((width, 1, rows), jnp.float32),
        grid=(rows // block,),
        in_specs=[
            pl.BlockSpec((width, depth), lambda i: (0, 0)),
            pl.BlockSpec((block, depth), lambda i: (i, 0)),
        ],
        out_specs=pl.BlockSpec((width, 1, block), lambda i: (0, 0, i)),
    )(amplitude, owned_all)
    return out.transpose(1, 2, 0)


def body(b_aux, occ_energies, vir_energies, owners, *, shards, n_aux, by_partials):
    local = b_aux[0]
    width = local.shape[1] // shards
    col_energy = (vir_energies[None, :] - occ_energies[:, None]).reshape(-1)
    shard_index = lax.axis_index(COLS)
    energy_mine = lax.dynamic_slice_in_dim(col_energy, shard_index * width, width, 0)
    owned, owner_energy = owner_columns(local, col_energy, owners, width)
    owned_all = lax.all_gather(owned, COLS, axis=0, tiled=True)
    if by_partials:
        coupling = coupling_by_partials(local, owned, shards, width)
        coupling = exchange_sum(coupling, "aux", n_aux)
    else:
        coupling = coupling_by_columns(local, owned_all, shards, width, n_aux)
    denominator = energy_mine[:, None] + owner_energy[None, :]
    amplitude = (os_scale * coupling / denominator).astype(jnp.bfloat16)
    return gamma_rows_last(amplitude, owned_all)


def solution(mesh):
    shards = mesh.shape["col"] * mesh.shape["rep"]

    def run(b_aux, occ_energies, vir_energies, owners):
        ncol = b_aux.shape[2]
        partial_bytes = ncol * owners.shape[0] * (ncol // shards) * 4
        by_partials = partial_bytes <= PARTIAL_BYTES_MAX
        placed = (P(("groups", "aux"), COLS, None), P("groups"), P("groups"), P())
        return jax.shard_map(
            lambda *a: body(*a, shards=shards, n_aux=mesh.shape["aux"], by_partials=by_partials),
            mesh=mesh,
            in_specs=placed,
            out_specs=P(("groups", "aux"), None, COLS),
            check_vma=False,
        )(b_aux, occ_energies, vir_energies, owners)

    return run
```

```python
import jax
import jax.numpy as jnp
from jax import lax
from jax.experimental import pallas as pl
from jax.experimental.pallas import tpu as pltpu
from jax.sharding import PartitionSpec as P

os_scale = 1.3
COLS = ("col", "rep")
PARTIAL_BYTES_MAX = 0
LANES = 128
ROW_BLOCK = 2048


def owner_columns(local, col_energy, owners, width):
    owned = []
    owner_energy = []
    for step_index in range(owners.shape[0]):
        first = owners[step_index] * width
        owned.append(lax.dynamic_slice_in_dim(local, first, width, 1))
        owner_energy.append(lax.dynamic_slice_in_dim(col_energy, first, width, 0))
    return jnp.concatenate(owned, axis=1), jnp.concatenate(owner_energy, axis=0)


def coupling_by_partials(local, owned, shards, width):
    rows = local.shape[0]
    blocked = local.reshape(rows, shards, width)
    partial_value = lax.dot_general(
        blocked, owned, (((0,), (0,)), ((), ())), preferred_element_type=jnp.float32
    )
    return lax.psum_scatter(partial_value, COLS, scatter_dimension=0, tiled=False)


def coupling_by_columns(local, owned_all, shards, width, n_aux):
    rows = local.shape[0]
    blocked = local.reshape(rows, shards, width).transpose(1, 0, 2)
    split = (width // LANES) * LANES
    edges = [0, split, width] if 0 < split < width else [0, width]
    pieces = []
    previous = None
    for first, last in zip(edges[:-1], edges[1:]):
        chunk = blocked[:, :, first:last]
        if previous is not None:
            chunk, _ = lax.optimization_barrier((chunk, previous))
        moved = lax.all_to_all(chunk, COLS, split_axis=0, concat_axis=0, tiled=True)
        previous = lax.dot_general(
            moved.reshape(shards * rows, last - first), owned_all, (((0,), (0,)), ((), ())),
            preferred_element_type=jnp.float32,
        )
        pieces.append(exchange_sum(previous, "aux", n_aux))
    return pieces


def exchange_sum(value, axis, size):
    total = value
    for step in range(1, size):
        total = total + lax.ppermute(value, axis, [(i, (i + step) % size) for i in range(size)])
    return total


def gamma_kernel(*refs):
    n_pieces = (len(refs) - 3) // 2
    owner_ref, owned_ref, out_ref = refs[-3], refs[-2], refs[-1]
    first = 0
    for index in range(n_pieces):
        coupling_ref, energy_ref = refs[2 * index], refs[2 * index + 1]
        amplitude = (
            os_scale * coupling_ref[...] / (energy_ref[...] + owner_ref[...])
        ).astype(jnp.bfloat16)
        last = first + coupling_ref.shape[0]
        out_ref[first:last, 0, :] = lax.dot_general(
            amplitude, owned_ref[...], (((1,), (1,)), ((), ())),
            preferred_element_type=jnp.float32,
        )
        first = last


def gamma_rows_last(pieces, energy_mine, owner_energy, owned_all):
    width = energy_mine.shape[0]
    depth = owner_energy.shape[0]
    rows = owned_all.shape[0]
    block = ROW_BLOCK if rows % ROW_BLOCK == 0 else rows
    operands = []
    in_specs = []
    first = 0
    for piece in pieces:
        last = first + piece.shape[0]
        operands += [piece, energy_mine[first:last, None]]
        in_specs += [
            pl.BlockSpec(piece.shape, lambda i: (0, 0)),
            pl.BlockSpec((last - first, 1), lambda i: (0, 0)),
        ]
        first = last
    operands += [owner_energy[None, :], owned_all]
    in_specs += [
        pl.BlockSpec((1, depth), lambda i: (0, 0)),
        pl.BlockSpec((block, depth), lambda i: (i, 0)),
    ]
    out = pl.pallas_call(
        gamma_kernel,
        out_shape=jax.ShapeDtypeStruct((width, 1, rows), jnp.float32),
        grid=(rows // block,),
        in_specs=in_specs,
        out_specs=pl.BlockSpec((width, 1, block), lambda i: (0, 0, i)),
    )(*operands)
    return out.transpose(1, 2, 0)


def body(b_aux, occ_energies, vir_energies, owners, *, shards, n_aux, by_partials):
    local = b_aux[0]
    width = local.shape[1] // shards
    col_energy = (vir_energies[None, :] - occ_energies[:, None]).reshape(-1)
    shard_index = lax.axis_index(COLS)
    energy_mine = lax.dynamic_slice_in_dim(col_energy, shard_index * width, width, 0)
    owned, owner_energy = owner_columns(local, col_energy, owners, width)
    owned_all = lax.all_gather(owned, COLS, axis=0, tiled=True)
    if by_partials:
        coupling = coupling_by_partials(local, owned, shards, width)
        pieces = [exchange_sum(coupling, "aux", n_aux)]
    else:
        pieces = coupling_by_columns(local, owned_all, shards, width, n_aux)
    return gamma_rows_last(pieces, energy_mine, owner_energy, owned_all)


def solution(mesh):
    shards = mesh.shape["col"] * mesh.shape["rep"]

    def run(b_aux, occ_energies, vir_energies, owners):
        ncol = b_aux.shape[2]
        partial_bytes = ncol * owners.shape[0] * (ncol // shards) * 4
        by_partials = partial_bytes <= PARTIAL_BYTES_MAX
        placed = (P(("groups", "aux"), COLS, None), P("groups"), P("groups"), P())
        return jax.shard_map(
            lambda *a: body(*a, shards=shards, n_aux=mesh.shape["aux"], by_partials=by_partials),
            mesh=mesh,
            in_specs=placed,
            out_specs=P(("groups", "aux"), None, COLS),
            check_vma=False,
        )(b_aux, occ_energies, vir_energies, owners)

    return run
```

```python
import jax
import jax.numpy as jnp
from jax import lax
from jax.experimental import pallas as pl
from jax.experimental.pallas import tpu as pltpu
from jax.sharding import PartitionSpec as P

os_scale = 1.3
COLS = ("col", "rep")
PARTIAL_BYTES_MAX = 0
LANES = 128
ROW_BLOCK = 2048


def owner_columns(local, col_energy, owners, width):
    owned = []
    owner_energy = []
    for step_index in range(owners.shape[0]):
        first = owners[step_index] * width
        owned.append(lax.dynamic_slice_in_dim(local, first, width, 1))
        owner_energy.append(lax.dynamic_slice_in_dim(col_energy, first, width, 0))
    return jnp.concatenate(owned, axis=1), jnp.concatenate(owner_energy, axis=0)


def coupling_by_partials(local, owned, shards, width):
    rows = local.shape[0]
    blocked = local.reshape(rows, shards, width)
    partial_value = lax.dot_general(
        blocked, owned, (((0,), (0,)), ((), ())), preferred_element_type=jnp.float32
    )
    return lax.psum_scatter(partial_value, COLS, scatter_dimension=0, tiled=False)


def coupling_by_columns(local, owned_all, shards, width, n_aux):
    rows = local.shape[0]
    blocked = local.reshape(rows, shards, width).transpose(1, 0, 2)
    split = (width // LANES) * LANES
    edges = [0, split, width] if 0 < split < width else [0, width]
    pieces = []
    previous = None
    for first, last in zip(edges[:-1], edges[1:]):
        chunk = blocked[:, :, first:last]
        if previous is not None:
            chunk, _ = lax.optimization_barrier((chunk, previous))
        moved = lax.all_to_all(chunk, COLS, split_axis=0, concat_axis=0, tiled=True)
        previous = coupling_blocks(moved, owned_all)
        pieces.append(exchange_sum(previous, "aux", n_aux))
    return jnp.concatenate(pieces, axis=0)


def coupling_kernel(moved_ref, owned_ref, out_ref):
    @pl.when(pl.program_id(0) == 0)
    def _():
        out_ref[...] = jnp.zeros_like(out_ref)

    out_ref[...] += lax.dot_general(
        moved_ref[0], owned_ref[...], (((0,), (0,)), ((), ())), preferred_element_type=jnp.float32
    )


def coupling_blocks(moved, owned_all):
    blocks, rows, width = moved.shape
    depth = owned_all.shape[1]
    return pl.pallas_call(
        coupling_kernel,
        out_shape=jax.ShapeDtypeStruct((width, depth), jnp.float32),
        grid=(blocks,),
        in_specs=[
            pl.BlockSpec((1, rows, width), lambda i: (i, 0, 0)),
            pl.BlockSpec((rows, depth), lambda i: (i, 0)),
        ],
        out_specs=pl.BlockSpec((width, depth), lambda i: (0, 0)),
    )(moved, owned_all)


def exchange_sum(value, axis, size):
    total = value
    for step in range(1, size):
        total = total + lax.ppermute(value, axis, [(i, (i + step) % size) for i in range(size)])
    return total


def gamma_kernel(amp_ref, owned_ref, out_ref):
    out_ref[:, 0, :] = lax.dot_general(
        amp_ref[...], owned_ref[...], (((1,), (1,)), ((), ())), preferred_element_type=jnp.float32
    )


def gamma_rows_last(amplitude, owned_all):
    width, depth = amplitude.shape
    rows = owned_all.shape[0]
    block = ROW_BLOCK if rows % ROW_BLOCK == 0 else rows
    out = pl.pallas_call(
        gamma_kernel,
        out_shape=jax.ShapeDtypeStruct((width, 1, rows), jnp.float32),
        grid=(rows // block,),
        in_specs=[
            pl.BlockSpec((width, depth), lambda i: (0, 0)),
            pl.BlockSpec((block, depth), lambda i: (i, 0)),
        ],
        out_specs=pl.BlockSpec((width, 1, block), lambda i: (0, 0, i)),
    )(amplitude, owned_all)
    return out.transpose(1, 2, 0)


def body(b_aux, occ_energies, vir_energies, owners, *, shards, n_aux, by_partials):
    local = b_aux[0]
    width = local.shape[1] // shards
    col_energy = (vir_energies[None, :] - occ_energies[:, None]).reshape(-1)
    shard_index = lax.axis_index(COLS)
    energy_mine = lax.dynamic_slice_in_dim(col_energy, shard_index * width, width, 0)
    owned, owner_energy = owner_columns(local, col_energy, owners, width)
    owned_all = lax.all_gather(owned, COLS, axis=0, tiled=True)
    if by_partials:
        coupling = coupling_by_partials(local, owned, shards, width)
        coupling = exchange_sum(coupling, "aux", n_aux)
    else:
        coupling = coupling_by_columns(local, owned_all, shards, width, n_aux)
    denominator = energy_mine[:, None] + owner_energy[None, :]
    amplitude = (os_scale * coupling / denominator).astype(jnp.bfloat16)
    return gamma_rows_last(amplitude, owned_all)


def solution(mesh):
    shards = mesh.shape["col"] * mesh.shape["rep"]

    def run(b_aux, occ_energies, vir_energies, owners):
        ncol = b_aux.shape[2]
        partial_bytes = ncol * owners.shape[0] * (ncol // shards) * 4
        by_partials = partial_bytes <= PARTIAL_BYTES_MAX
        placed = (P(("groups", "aux"), COLS, None), P("groups"), P("groups"), P())
        return jax.shard_map(
            lambda *a: body(*a, shards=shards, n_aux=mesh.shape["aux"], by_partials=by_partials),
            mesh=mesh,
            in_specs=placed,
            out_specs=P(("groups", "aux"), None, COLS),
            check_vma=False,
        )(b_aux, occ_energies, vir_energies, owners)

    return run
```

```python
import jax
import jax.numpy as jnp
from jax import lax
from jax.experimental import pallas as pl
from jax.experimental.pallas import tpu as pltpu
from jax.sharding import PartitionSpec as P

os_scale = 1.3
COLS = ("col", "rep")
PARTIAL_BYTES_MAX = 0
LANES = 128
ROW_BLOCK = 4096


def owner_columns(local, col_energy, owners, width):
    owned = []
    owner_energy = []
    for step_index in range(owners.shape[0]):
        first = owners[step_index] * width
        owned.append(lax.dynamic_slice_in_dim(local, first, width, 1))
        owner_energy.append(lax.dynamic_slice_in_dim(col_energy, first, width, 0))
    return jnp.concatenate(owned, axis=1), jnp.concatenate(owner_energy, axis=0)


def coupling_by_partials(local, owned, shards, width):
    rows = local.shape[0]
    blocked = local.reshape(rows, shards, width)
    partial_value = lax.dot_general(
        blocked, owned, (((0,), (0,)), ((), ())), preferred_element_type=jnp.float32
    )
    return lax.psum_scatter(partial_value, COLS, scatter_dimension=0, tiled=False)


def coupling_by_columns(local, owned_all, shards, width, n_aux):
    rows = local.shape[0]
    blocked = local.reshape(rows, shards, width).transpose(1, 0, 2)
    split = (width // LANES) * LANES
    edges = [0, split, width] if 0 < split < width else [0, width]
    pieces = []
    previous = None
    for first, last in zip(edges[:-1], edges[1:]):
        chunk = blocked[:, :, first:last]
        if previous is not None:
            chunk, _ = lax.optimization_barrier((chunk, previous))
        moved = lax.all_to_all(chunk, COLS, split_axis=0, concat_axis=0, tiled=True)
        previous = lax.dot_general(
            moved.reshape(shards * rows, last - first), owned_all, (((0,), (0,)), ((), ())),
            preferred_element_type=jnp.float32,
        )
        pieces.append(exchange_sum(previous, "aux", n_aux))
    return jnp.concatenate(pieces, axis=0)


def exchange_sum(value, axis, size):
    total = value
    for step in range(1, size):
        total = total + lax.ppermute(value, axis, [(i, (i + step) % size) for i in range(size)])
    return total


def gamma_kernel(amp_ref, owned_ref, out_ref):
    out_ref[:, 0, :] = lax.dot_general(
        amp_ref[...], owned_ref[...], (((1,), (1,)), ((), ())), preferred_element_type=jnp.float32
    )


def gamma_rows_last(amplitude, owned_all):
    width, depth = amplitude.shape
    rows = owned_all.shape[0]
    block = ROW_BLOCK if rows % ROW_BLOCK == 0 else rows
    out = pl.pallas_call(
        gamma_kernel,
        out_shape=jax.ShapeDtypeStruct((width, 1, rows), jnp.float32),
        grid=(rows // block,),
        in_specs=[
            pl.BlockSpec((width, depth), lambda i: (0, 0)),
            pl.BlockSpec((block, depth), lambda i: (i, 0)),
        ],
        out_specs=pl.BlockSpec((width, 1, block), lambda i: (0, 0, i)),
    )(amplitude, owned_all)
    return out.transpose(1, 2, 0)


def body(b_aux, occ_energies, vir_energies, owners, *, shards, n_aux, by_partials):
    local = b_aux[0]
    width = local.shape[1] // shards
    col_energy = (vir_energies[None, :] - occ_energies[:, None]).reshape(-1)
    shard_index = lax.axis_index(COLS)
    energy_mine = lax.dynamic_slice_in_dim(col_energy, shard_index * width, width, 0)
    owned, owner_energy = owner_columns(local, col_energy, owners, width)
    owned_all = lax.all_gather(owned, COLS, axis=0, tiled=True)
    if by_partials:
        coupling = coupling_by_partials(local, owned, shards, width)
        coupling = exchange_sum(coupling, "aux", n_aux)
    else:
        coupling = coupling_by_columns(local, owned_all, shards, width, n_aux)
    denominator = energy_mine[:, None] + owner_energy[None, :]
    amplitude = (os_scale * coupling / denominator).astype(jnp.bfloat16)
    return gamma_rows_last(amplitude, owned_all)


def solution(mesh):
    shards = mesh.shape["col"] * mesh.shape["rep"]

    def run(b_aux, occ_energies, vir_energies, owners):
        ncol = b_aux.shape[2]
        partial_bytes = ncol * owners.shape[0] * (ncol // shards) * 4
        by_partials = partial_bytes <= PARTIAL_BYTES_MAX
        placed = (P(("groups", "aux"), COLS, None), P("groups"), P("groups"), P())
        return jax.shard_map(
            lambda *a: body(*a, shards=shards, n_aux=mesh.shape["aux"], by_partials=by_partials),
            mesh=mesh,
            in_specs=placed,
            out_specs=P(("groups", "aux"), None, COLS),
            check_vma=False,
        )(b_aux, occ_energies, vir_energies, owners)

    return run
```
